512 devices in a mesh: ctx: 128 (over x, z, core), head: 4 (over y).
Axes of the slice: x: 4, y: 4, z: 16, core: 2. Of those that a mesh axis runs over, the one named last changes fastest.
Arguments:
- lin_query: bfloat16 [32768, 256], P('ctx', 'head'), may hold values from -4 to 4
- lin_key: bfloat16 [32768, 256], P('ctx', 'head'), may hold values from -3 to 3
- lin_values: bfloat16 [32768, 2048], P('ctx', 'head'), may hold values from -43 to 43
- win_query: bfloat16 [32768, 2048], P('ctx', 'head'), may hold values from -30 to 30
- win_key: bfloat16 [32768, 2048], P('ctx', 'head'), may hold values from -30 to 30
- win_value: bfloat16 [32768, 2048], P('ctx', 'head'), may hold values from -4 to 4
- conv_weight: bfloat16 [3, 2048], P(None, 'head'), may hold values from -3 to 3
- head_gain: float32 [2048], P('head'), may hold values from 0.7 to 12.6
Outputs:
- mixed_out: bfloat16 [32768, 2048], P('ctx', 'head')
The draws below stay inside these ranges and needn't reach their ends.
All inputs are finite; a program needn't handle non-finite values.
Results may differ from the reference program's by a relative error of at most 0.0019.
Values may be sent and summed in bfloat16 or wider, within the bound.
No kernel may reach another device: no remote copies, remote signals or barrier semaphores. Data moves between devices by JAX's collectives and lax.ppermute only.
A program may use at most 192 MiB of HBM per device.

```python
import math
import jax
import jax.numpy as jnp
from jax import lax

HEADS = 16
FDIM = 16
VDIM = 128
WIN = 64
TAPS = 3
TOK_DEV = 256
D = 2048
FEAT = 273
TOKENS = 32768


def window_pair(key):
    base = jax.random.fold_in(key, 404)
    query = jnp.clip(jax.random.normal(jax.random.fold_in(base, 1), (TOKENS, D), jnp.float32), -4.0, 4.0)
    keys = jnp.clip(jax.random.normal(jax.random.fold_in(base, 2), (TOKENS, D), jnp.float32), -4.0, 4.0)
    return (query.astype(jnp.bfloat16), keys.astype(jnp.bfloat16))


def draw_win_query(key, part):
    return window_pair(key)[0]


def draw_win_key(key, part):
    return window_pair(key)[1]


def linear_keys(key):
    base = jax.random.fold_in(key, 707)
    keys = jnp.clip(jax.random.normal(base, (TOKENS, HEADS * FDIM), jnp.float32), -3.0, 3.0)
    return keys.astype(jnp.bfloat16)


def draw_lin_key(key, part):
    return linear_keys(key)


def draw_lin_values(key, part):
    base = jax.random.fold_in(key, 505)
    keys = linear_keys(key).astype(jnp.float32)
    column = jnp.arange(D, dtype=jnp.int32)
    head_of = column // VDIM
    channel = column % VDIM
    first = head_of * FDIM + channel % FDIM
    second = head_of * FDIM + (channel // FDIM + channel + head_of) % FDIM
    product = keys[:, first] * keys[:, second]
    noise = jnp.clip(jax.random.normal(jax.random.fold_in(base, 1), (TOKENS, D), jnp.float32), -4.0, 4.0)
    offsets = 3.0 * jnp.clip(jax.random.normal(jax.random.fold_in(base, 2), (TOKENS // TOK_DEV, D), jnp.float32), -4.0, 4.0)
    rows = jnp.arange(TOKENS) // TOK_DEV
    return (3.0 * product + noise + offsets[rows]).astype(jnp.bfloat16)


def draw_head_gain(key, part):
    base = jax.random.fold_in(key, 606)
    ratio = 3.0
    column = jnp.arange(D).astype(jnp.float32)
    rising = jnp.exp(jnp.log(ratio) * column / (D - 1))
    jitter = jax.random.uniform(base, (D,), jnp.float32, 0.7, 1.4)
    return rising * jitter


def level_of(rng, shape, pieces, low, high):
    level, own = 1.0, jax.random.fold_in(rng, 6)
    for dim, shards_of in pieces:
        steps = jnp.exp(jax.random.uniform(jax.random.fold_in(own, dim), (shards_of,), jnp.float32, low / len(pieces), high / len(pieces)))
        level = level * jnp.repeat(steps, shape[dim] // shards_of).reshape([-1 if axis == dim else 1 for axis in range(len(shape))])
    return level


def scatter_about(stream_key, extent, spread, most, split=(), held_as=jnp.bfloat16):
    array = jax.random.normal(stream_key, extent, jnp.float32) * spread
    if len(split) > 0:
        array = level_of(stream_key, extent, split, -0.22, 0.18) * array
    return jnp.clip(array, min=-most, max=most).astype(held_as)


def setup_inputs(seed: int = 0) -> dict:
    key_list = jax.random.split(jax.random.key(seed), 9)
    lin_query = scatter_about(key_list[0], (TOKENS, HEADS * FDIM), 1.0, 4.0, ((0, 128), (1, 4)))
    lin_key = draw_lin_key(jax.random.fold_in(key_list[8], 71), 0)
    lin_values = draw_lin_values(jax.random.fold_in(key_list[8], 71), 0)
    win_query = draw_win_query(jax.random.fold_in(key_list[8], 71), 0)
    win_key = draw_win_key(jax.random.fold_in(key_list[8], 71), 0)
    win_value = scatter_about(key_list[5], (TOKENS, D), 1.0, 4.0, ((0, 128), (1, 4)))
    conv_weight = scatter_about(key_list[6], (TAPS, D), 0.6, 3.0, ((1, 4),))
    head_gain = draw_head_gain(jax.random.fold_in(key_list[8], 71), 0)
    return dict(lin_query=lin_query, lin_key=lin_key, lin_values=lin_values, win_query=win_query, win_key=win_key, win_value=win_value, conv_weight=conv_weight, head_gain=head_gain)


def features_outer(x_tok):
    xt = jnp.transpose(x_tok.astype(jnp.float32), (1, 2, 0))
    heads, fdim, count = xt.shape
    ones = jnp.ones((heads, 1, count), jnp.float32)
    outer = (xt[:, :, None, :] * xt[:, None, :, :]).reshape(heads, fdim * fdim, count) * (1.0 / math.sqrt(32.0))
    return jnp.concatenate([ones, xt * 0.5, outer], axis=1)

def window_slab(query, key_ext, value_ext, start):
    count, width = query.shape
    heads = width // VDIM
    blocks = count // WIN
    qb = query.astype(jnp.float32).reshape(blocks, WIN, heads, VDIM)
    prev_k = key_ext[:count].astype(jnp.float32).reshape(blocks, WIN, heads, VDIM)
    this_k = key_ext[WIN:].astype(jnp.float32).reshape(blocks, WIN, heads, VDIM)
    prev_v = value_ext[:count].astype(jnp.float32).reshape(blocks, WIN, heads, VDIM)
    this_v = value_ext[WIN:].astype(jnp.float32).reshape(blocks, WIN, heads, VDIM)
    keys = jnp.concatenate([prev_k, this_k], axis=1)
    vals = jnp.concatenate([prev_v, this_v], axis=1)
    scores = jnp.einsum('bihe,bjhe->bhij', qb, keys) * (1.0 / math.sqrt(VDIM))
    rows_i = jnp.arange(WIN, dtype=jnp.int32)[:, None]
    cols_j = jnp.arange(2 * WIN, dtype=jnp.int32)[None, :]
    block_ids = jnp.arange(blocks, dtype=jnp.int32)[:, None, None]
    position = start + block_ids * WIN + cols_j[None] - WIN
    allowed = (cols_j > rows_i)[None] & (cols_j <= rows_i + WIN)[None] & (position >= 0)
    allowed = allowed[:, None]
    top = lax.optimization_barrier(jnp.max(jnp.where(allowed, scores, jnp.float32(-1e+30)), axis=-1, keepdims=True))
    prob = jnp.where(allowed, jnp.exp(scores - top), jnp.float32(0.0))
    total = lax.optimization_barrier(jnp.sum(prob, axis=-1))
    prob_bf = lax.optimization_barrier(prob.astype(jnp.bfloat16)).astype(jnp.float32)
    out = jnp.einsum('bhij,bjhe->bihe', prob_bf, vals)
    out = out / jnp.transpose(total, (0, 2, 1))[..., None]
    return out.reshape(count, width)

def conv_slab(value_ext, weight, count):
    ext = value_ext.astype(jnp.float32)
    taps = weight.astype(jnp.float32)
    acc = jnp.zeros((count, ext.shape[1]), jnp.float32)
    for tap in range(TAPS):
        acc = acc + taps[tap][None, :] * ext[WIN - tap:WIN - tap + count]
    return acc

def reference(lin_query, lin_key, lin_values, win_query, win_key, win_value, conv_weight, head_gain):
    slabs = TOKENS // TOK_DEV
    pad_rows = jnp.zeros((WIN, D), jnp.bfloat16)
    key_pad = jnp.concatenate([pad_rows, win_key], axis=0)
    value_pad = jnp.concatenate([pad_rows, win_value], axis=0)
    gain = head_gain.astype(jnp.float32)

    def step(carry, slab):
        state, normer = carry
        begin = (slab * TOK_DEV).astype(jnp.int32)
        qs = lax.dynamic_slice_in_dim(lin_query, begin, TOK_DEV, 0).reshape(TOK_DEV, HEADS, FDIM)
        ks = lax.dynamic_slice_in_dim(lin_key, begin, TOK_DEV, 0).reshape(TOK_DEV, HEADS, FDIM)
        vs = lax.dynamic_slice_in_dim(lin_values, begin, TOK_DEV, 0).reshape(TOK_DEV, HEADS, VDIM)
        q32 = qs.astype(jnp.float32)
        k32 = ks.astype(jnp.float32)
        v32 = vs.astype(jnp.float32)
        sim = jnp.einsum('thf,shf->hts', q32, k32) * 0.25
        causal = jnp.arange(TOK_DEV, dtype=jnp.int32)[:, None] >= jnp.arange(TOK_DEV, dtype=jnp.int32)[None, :]
        weights = jnp.where(causal[None], 1.0 + sim + 0.5 * sim * sim, jnp.float32(0.0))
        inner_den = lax.optimization_barrier(jnp.sum(weights, axis=-1))
        weights_bf = lax.optimization_barrier(weights.astype(jnp.bfloat16)).astype(jnp.float32)
        inner_num = jnp.einsum('hts,shv->htv', weights_bf, v32)
        phi_q = features_outer(qs)
        phi_k = features_outer(ks)
        numer = inner_num + jnp.einsum('hft,hfv->htv', phi_q, state, precision=lax.Precision.HIGHEST)
        denom = inner_den + jnp.einsum('hft,hf->ht', phi_q, normer, precision=lax.Precision.HIGHEST)
        lin = jnp.transpose(numer / denom[..., None], (1, 0, 2)).reshape(TOK_DEV, D)
        state = state + jnp.einsum('hft,thv->hfv', phi_k, v32, precision=lax.Precision.HIGHEST)
        normer = normer + lax.optimization_barrier(jnp.sum(phi_k, axis=-1))
        wq = lax.dynamic_slice_in_dim(win_query, begin, TOK_DEV, 0)
        wk = lax.dynamic_slice_in_dim(key_pad, begin, TOK_DEV + WIN, 0)
        wv = lax.dynamic_slice_in_dim(value_pad, begin, TOK_DEV + WIN, 0)
        win = window_slab(wq, wk, wv, begin)
        conv = conv_slab(wv, conv_weight, TOK_DEV)
        mixed = gain[None, :] * (lin + win + conv)
        msq = lax.optimization_barrier(jnp.sum(mixed * mixed, axis=-1)) / D
        out = (mixed * lax.rsqrt(msq + 1e-06)[:, None]).astype(jnp.bfloat16)
        return ((state, normer), out)
    start_state = jnp.zeros((HEADS, FEAT, VDIM), jnp.float32)
    start_norm = jnp.zeros((HEADS, FEAT), jnp.float32)
    carry, outs = lax.scan(step, (start_state, start_norm), jnp.arange(slabs, dtype=jnp.int32))
    return outs.reshape(TOKENS, D)
```

```python
import math

import numpy as np
import jax
import jax.numpy as jnp
from jax import lax
from jax.sharding import PartitionSpec as P

FDIM = 16
VDIM = 128
WIN = 64
TAPS = 3
D = 2048
HIGH = lax.Precision.HIGHEST


def passed_along(shard, axis, by):
    length = lax.axis_size(axis)
    pairs = [(i, i + by) for i in range(length) if 0 <= i + by < length]
    return lax.ppermute(shard, axis, pairs)


def compact_features(x_tok, doubled):
    xt = jnp.transpose(x_tok.astype(jnp.float32), (1, 2, 0))
    heads, fdim, count = xt.shape
    ones = jnp.ones((heads, 1, count), jnp.float32)
    rows = []
    for i in range(fdim):
        part = xt[:, i : i + 1, :] * xt[:, i:, :]
        if doubled:
            scale = np.full((1, fdim - i, 1), 2.0, np.float32)
            scale[0, 0, 0] = 1.0
            part = part * scale
        rows.append(part)
    outer = jnp.concatenate(rows, axis=1) * (1.0 / math.sqrt(32.0))
    return jnp.concatenate([ones, xt * 0.5, outer], axis=1)


def exclusive_prefix(flat, axis):
    size = lax.axis_size(axis)
    chunks = flat.reshape(size, -1)
    recv = lax.all_to_all(chunks, axis, 0, 0, tiled=True)
    lower = jnp.asarray(np.tril(np.ones((size, size), np.float32), -1))
    pref = jnp.dot(lower, recv, precision=HIGH, preferred_element_type=jnp.float32)
    back = lax.all_to_all(pref, axis, 0, 0, tiled=True)
    return back.reshape(-1)


def window_slab(query, key_ext, value_ext, start):
    count, width = query.shape
    heads = width // VDIM
    blocks = count // WIN
    qb = query.reshape(blocks, WIN, heads, VDIM)
    keys = jnp.concatenate(
        [
            key_ext[:count].reshape(blocks, WIN, heads, VDIM),
            key_ext[WIN:].reshape(blocks, WIN, heads, VDIM),
        ],
        axis=1,
    )
    vals = jnp.concatenate(
        [
            value_ext[:count].reshape(blocks, WIN, heads, VDIM),
            value_ext[WIN:].reshape(blocks, WIN, heads, VDIM),
        ],
        axis=1,
    )
    scores = jnp.einsum("bihe,bjhe->bhij", qb, keys, preferred_element_type=jnp.float32) * (
        1.0 / math.sqrt(VDIM)
    )
    rows_i = jnp.arange(WIN, dtype=jnp.int32)[:, None]
    cols_j = jnp.arange(2 * WIN, dtype=jnp.int32)[None, :]
    block_ids = jnp.arange(blocks, dtype=jnp.int32)[:, None, None]
    position = start + block_ids * WIN + cols_j[None] - WIN
    allowed = (cols_j > rows_i)[None] & (cols_j <= rows_i + WIN)[None] & (position >= 0)
    allowed = allowed[:, None]
    top = jnp.max(jnp.where(allowed, scores, jnp.float32(-1e30)), axis=-1, keepdims=True)
    prob = jnp.where(allowed, jnp.exp(scores - top), jnp.float32(0.0))
    total = jnp.sum(prob, axis=-1)
    out = jnp.einsum(
        "bhij,bjhe->bihe", prob.astype(jnp.bfloat16), vals, preferred_element_type=jnp.float32
    )
    out = out / jnp.transpose(total, (0, 2, 1))[..., None]
    return out.reshape(count, width)


def inner_causal(queries, keys, values):
    count = queries.shape[0]
    sim = jnp.einsum("thf,shf->hts", queries, keys, preferred_element_type=jnp.float32) * 0.25
    row_pos = jnp.arange(count, dtype=jnp.int32)
    causal = row_pos[:, None] >= row_pos[None, :]
    weights = jnp.where(causal[None], 1.0 + sim + 0.5 * sim * sim, jnp.float32(0.0))
    denom_parts = jnp.sum(weights, axis=-1)
    numer_parts = jnp.einsum(
        "hts,shv->htv", weights.astype(jnp.bfloat16), values, preferred_element_type=jnp.float32
    )
    return (numer_parts, denom_parts)


def head_sum(part, axis):
    size = lax.axis_size(axis)
    total = part
    step = 1
    while step < size:
        pairs = [(i, i ^ step) for i in range(size)]
        total = total + lax.ppermute(total, axis, pairs)
        step *= 2
    return total


def body(lin_query, lin_key, lin_values, win_query, win_key, win_value, conv_weight, head_gain):
    count = lin_query.shape[0]
    heads = lin_query.shape[1] // FDIM
    queries = lin_query.reshape(count, heads, FDIM)
    keys = lin_key.reshape(count, heads, FDIM)
    values = lin_values.reshape(count, heads, VDIM)
    values32 = values.astype(jnp.float32)
    phi_q = compact_features(queries, True)
    phi_k = compact_features(keys, False)
    feat = phi_k.shape[1]
    local_state = jnp.einsum("hft,thv->hfv", phi_k, values32, precision=HIGH)
    local_norm = jnp.sum(phi_k, axis=-1)
    size = lax.axis_size("ctx")
    packed = jnp.concatenate([local_state.reshape(-1), local_norm.reshape(-1)])
    used = packed.shape[0]
    quantum = size * 128
    padded = -(-used // quantum) * quantum
    packed = jnp.pad(packed, (0, padded - used))
    prior = exclusive_prefix(packed, "ctx")
    split = heads * feat * VDIM
    prior_state = prior[:split].reshape(heads, feat, VDIM)
    prior_norm = prior[split:used].reshape(heads, feat)
    start = lax.axis_index("ctx") * count
    rims = passed_along((win_key[count - WIN :], win_value[count - WIN :]), "ctx", 1)
    key_ext = jnp.concatenate([rims[0], win_key], axis=0)
    value_ext = jnp.concatenate([rims[1], win_value], axis=0)
    window_out = window_slab(win_query, key_ext, value_ext, start)
    taps = conv_weight.astype(jnp.float32)
    value_f32 = value_ext.astype(jnp.float32)
    conv_out = jnp.zeros((count, value_ext.shape[1]), jnp.float32)
    for tap in range(TAPS):
        conv_out = conv_out + taps[tap][None, :] * value_f32[WIN - tap : WIN - tap + count]
    inner_num, inner_den = inner_causal(queries, keys, values)
    numer = inner_num + jnp.einsum("hft,hfv->htv", phi_q, prior_state, precision=HIGH)
    denom = inner_den + jnp.einsum("hft,hf->ht", phi_q, prior_norm, precision=HIGH)
    lin_out = jnp.transpose(numer / denom[..., None], (1, 0, 2)).reshape(count, heads * VDIM)
    mixed = head_gain[None, :] * (lin_out + window_out + conv_out)
    squares = head_sum(jnp.sum(mixed * mixed, axis=-1), "head")
    msq = squares / D
    return (mixed * lax.rsqrt(msq + 1e-06)[:, None]).astype(jnp.bfloat16)


def solution(mesh):
    placed = (
        P("ctx", "head"),
        P("ctx", "head"),
        P("ctx", "head"),
        P("ctx", "head"),
        P("ctx", "head"),
        P("ctx", "head"),
        P(None, "head"),
        P("head"),
    )
    return jax.shard_map(
        body, mesh=mesh, in_specs=placed, out_specs=P("ctx", "head"), check_vma=False
    )
```

```python
import math

import numpy as np
import jax
import jax.numpy as jnp
from jax import lax
from jax.sharding import PartitionSpec as P

FDIM = 16
VDIM = 128
WIN = 64
TAPS = 3
D = 2048
HIGH = lax.Precision.HIGHEST


def passed_along(shard, axis, by):
    length = lax.axis_size(axis)
    pairs = [(i, i + by) for i in range(length) if 0 <= i + by < length]
    return lax.ppermute(shard, axis, pairs)


def features_outer(x_tok):
    xt = jnp.transpose(x_tok.astype(jnp.float32), (1, 2, 0))
    heads, fdim, count = xt.shape
    ones = jnp.ones((heads, 1, count), jnp.float32)
    outer = (xt[:, :, None, :] * xt[:, None, :, :]).reshape(heads, fdim * fdim, count) * (
        1.0 / math.sqrt(32.0)
    )
    return jnp.concatenate([ones, xt * 0.5, outer], axis=1)


def fold_matrix(fdim, doubled):
    full = 1 + fdim + fdim * fdim
    pairs = [(i, j) for i in range(fdim) for j in range(i, fdim)]
    fold = np.zeros((1 + fdim + len(pairs), full), np.float32)
    for r in range(1 + fdim):
        fold[r, r] = 1.0
    for r, (i, j) in enumerate(pairs):
        fold[1 + fdim + r, 1 + fdim + i * fdim + j] = 1.0
        if doubled and i != j:
            fold[1 + fdim + r, 1 + fdim + j * fdim + i] = 1.0
    return jnp.asarray(fold)


def compact_features(x_tok, doubled):
    full = features_outer(x_tok)
    fold = fold_matrix(x_tok.shape[-1], doubled)
    return jnp.einsum("cf,hft->hct", fold, full, precision=HIGH)


def exclusive_prefix(flat, axis):
    size = lax.axis_size(axis)
    chunks = flat.reshape(size, -1)
    recv = lax.all_to_all(chunks, axis, 0, 0, tiled=True)
    lower = jnp.asarray(np.tril(np.ones((size, size), np.float32), -1))
    pref = jnp.dot(lower, recv, precision=HIGH, preferred_element_type=jnp.float32)
    back = lax.all_to_all(pref, axis, 0, 0, tiled=True)
    return back.reshape(-1)


def window_slab(query, key_ext, value_ext, start):
    count, width = query.shape
    heads = width // VDIM
    blocks = count // WIN
    qb = query.reshape(blocks, WIN, heads, VDIM)
    keys = jnp.concatenate(
        [
            key_ext[:count].reshape(blocks, WIN, heads, VDIM),
            key_ext[WIN:].reshape(blocks, WIN, heads, VDIM),
        ],
        axis=1,
    )
    vals = jnp.concatenate(
        [
            value_ext[:count].reshape(blocks, WIN, heads, VDIM),
            value_ext[WIN:].reshape(blocks, WIN, heads, VDIM),
        ],
        axis=1,
    )
    scores = jnp.einsum("bihe,bjhe->bhij", qb, keys, preferred_element_type=jnp.float32) * (
        1.0 / math.sqrt(VDIM)
    )
    rows_i = jnp.arange(WIN, dtype=jnp.int32)[:, None]
    cols_j = jnp.arange(2 * WIN, dtype=jnp.int32)[None, :]
    block_ids = jnp.arange(blocks, dtype=jnp.int32)[:, None, None]
    position = start + block_ids * WIN + cols_j[None] - WIN
    allowed = (cols_j > rows_i)[None] & (cols_j <= rows_i + WIN)[None] & (position >= 0)
    allowed = allowed[:, None]
    top = jnp.max(jnp.where(allowed, scores, jnp.float32(-1e30)), axis=-1, keepdims=True)
    prob = jnp.where(allowed, jnp.exp(scores - top), jnp.float32(0.0))
    total = jnp.sum(prob, axis=-1)
    out = jnp.einsum(
        "bhij,bjhe->bihe", prob.astype(jnp.bfloat16), vals, preferred_element_type=jnp.float32
    )
    out = out / jnp.transpose(total, (0, 2, 1))[..., None]
    return out.reshape(count, width)


def inner_causal(queries, keys, values):
    count = queries.shape[0]
    sim = jnp.einsum("thf,shf->hts", queries, keys, preferred_element_type=jnp.float32) * 0.25
    row_pos = jnp.arange(count, dtype=jnp.int32)
    causal = row_pos[:, None] >= row_pos[None, :]
    weights = jnp.where(causal[None], 1.0 + sim + 0.5 * sim * sim, jnp.float32(0.0))
    denom_parts = jnp.sum(weights, axis=-1)
    numer_parts = jnp.einsum(
        "hts,shv->htv", weights.astype(jnp.bfloat16), values, preferred_element_type=jnp.float32
    )
    return (numer_parts, denom_parts)


def head_sum(part, axis):
    size = lax.axis_size(axis)
    total = part
    step = 1
    while step < size:
        pairs = [(i, i ^ step) for i in range(size)]
        total = total + lax.ppermute(total, axis, pairs)
        step *= 2
    return total


def body(lin_query, lin_key, lin_values, win_query, win_key, win_value, conv_weight, head_gain):
    count = lin_query.shape[0]
    heads = lin_query.shape[1] // FDIM
    queries = lin_query.reshape(count, heads, FDIM)
    keys = lin_key.reshape(count, heads, FDIM)
    values = lin_values.reshape(count, heads, VDIM)
    values32 = values.astype(jnp.float32)
    phi_q = compact_features(queries, True)
    phi_k = compact_features(keys, False)
    feat = phi_k.shape[1]
    local_state = jnp.einsum("hft,thv->hfv", phi_k, values32, precision=HIGH)
    local_norm = jnp.sum(phi_k, axis=-1)
    size = lax.axis_size("ctx")
    packed = jnp.concatenate([local_state.reshape(-1), local_norm.reshape(-1)])
    used = packed.shape[0]
    quantum = size * 128
    padded = -(-used // quantum) * quantum
    packed = jnp.pad(packed, (0, padded - used))
    prior = exclusive_prefix(packed, "ctx")
    split = heads * feat * VDIM
    prior_state = prior[:split].reshape(heads, feat, VDIM)
    prior_norm = prior[split:used].reshape(heads, feat)
    start = lax.axis_index("ctx") * count
    rims = passed_along((win_key[count - WIN :], win_value[count - WIN :]), "ctx", 1)
    key_ext = jnp.concatenate([rims[0], win_key], axis=0)
    value_ext = jnp.concatenate([rims[1], win_value], axis=0)
    window_out = window_slab(win_query, key_ext, value_ext, start)
    taps = conv_weight.astype(jnp.float32)
    value_f32 = value_ext.astype(jnp.float32)
    conv_out = jnp.zeros((count, value_ext.shape[1]), jnp.float32)
    for tap in range(TAPS):
        conv_out = conv_out + taps[tap][None, :] * value_f32[WIN - tap : WIN - tap + count]
    inner_num, inner_den = inner_causal(queries, keys, values)
    numer = inner_num + jnp.einsum("hft,hfv->htv", phi_q, prior_state, precision=HIGH)
    denom = inner_den + jnp.einsum("hft,hf->ht", phi_q, prior_norm, precision=HIGH)
    lin_out = jnp.transpose(numer / denom[..., None], (1, 0, 2)).reshape(count, heads * VDIM)
    mixed = head_gain[None, :] * (lin_out + window_out + conv_out)
    squares = head_sum(jnp.sum(mixed * mixed, axis=-1), "head")
    msq = squares / D
    return (mixed * lax.rsqrt(msq + 1e-06)[:, None]).astype(jnp.bfloat16)


def solution(mesh):
    placed = (
        P("ctx", "head"),
        P("ctx", "head"),
        P("ctx", "head"),
        P("ctx", "head"),
        P("ctx", "head"),
        P("ctx", "head"),
        P(None, "head"),
        P("head"),
    )
    return jax.shard_map(
        body, mesh=mesh, in_specs=placed, out_specs=P("ctx", "head"), check_vma=False
    )
```

```python
import math

import numpy as np
import jax
import jax.numpy as jnp
from jax import lax
from jax.sharding import Mesh, PartitionSpec as P

FDIM = 16
VDIM = 128
WIN = 64
TAPS = 3
D = 2048
HIGH = lax.Precision.HIGHEST


CTX = ("cx", "cz", "cc")


def passed_along(shard, axis, by):
    length = math.prod(lax.axis_size(a) for a in axis)
    pairs = [(i, i + by) for i in range(length) if 0 <= i + by < length]
    return lax.ppermute(shard, axis, pairs)


def features_outer(x_tok):
    xt = jnp.transpose(x_tok.astype(jnp.float32), (1, 2, 0))
    heads, fdim, count = xt.shape
    ones = jnp.ones((heads, 1, count), jnp.float32)
    outer = (xt[:, :, None, :] * xt[:, None, :, :]).reshape(heads, fdim * fdim, count) * (
        1.0 / math.sqrt(32.0)
    )
    return jnp.concatenate([ones, xt * 0.5, outer], axis=1)


def fold_matrix(fdim, doubled):
    full = 1 + fdim + fdim * fdim
    pairs = [(i, j) for i in range(fdim) for j in range(i, fdim)]
    fold = np.zeros((1 + fdim + len(pairs), full), np.float32)
    for r in range(1 + fdim):
        fold[r, r] = 1.0
    for r, (i, j) in enumerate(pairs):
        fold[1 + fdim + r, 1 + fdim + i * fdim + j] = 1.0
        if doubled and i != j:
            fold[1 + fdim + r, 1 + fdim + j * fdim + i] = 1.0
    return jnp.asarray(fold)


def compact_features(x_tok, doubled):
    full = features_outer(x_tok)
    fold = fold_matrix(x_tok.shape[-1], doubled)
    return jnp.einsum("cf,hft->hct", fold, full, precision=HIGH)


def masked_rows(rows, upto):
    keep = jnp.arange(rows.shape[0], dtype=jnp.int32)[:, None] < upto
    return jnp.sum(jnp.where(keep, rows, jnp.float32(0.0)), axis=0)


def exclusive_prefix(flat):
    cores = lax.axis_size("cc")
    core = lax.axis_index("cc")
    pair = lax.all_gather(flat, "cc")
    below_core = masked_rows(pair, core)
    chip = jnp.sum(pair, axis=0)
    share = lax.dynamic_index_in_dim(chip.reshape(cores, -1), core, 0, False)
    along_z = lax.all_gather(share, "cz")
    below_z = masked_rows(along_z, lax.axis_index("cz"))
    along_x = lax.all_gather(jnp.sum(along_z, axis=0), "cx")
    below_x = masked_rows(along_x, lax.axis_index("cx"))
    shares = lax.all_gather(below_x + below_z, "cc")
    return shares.reshape(-1) + below_core


def window_slab(query, key_ext, value_ext, start):
    count, width = query.shape
    heads = width // VDIM
    blocks = count // WIN
    qb = query.reshape(blocks, WIN, heads, VDIM)
    keys = jnp.concatenate(
        [
            key_ext[:count].reshape(blocks, WIN, heads, VDIM),
            key_ext[WIN:].reshape(blocks, WIN, heads, VDIM),
        ],
        axis=1,
    )
    vals = jnp.concatenate(
        [
            value_ext[:count].reshape(blocks, WIN, heads, VDIM),
            value_ext[WIN:].reshape(blocks, WIN, heads, VDIM),
        ],
        axis=1,
    )
    scores = jnp.einsum("bihe,bjhe->bhij", qb, keys, preferred_element_type=jnp.float32) * (
        1.0 / math.sqrt(VDIM)
    )
    rows_i = jnp.arange(WIN, dtype=jnp.int32)[:, None]
    cols_j = jnp.arange(2 * WIN, dtype=jnp.int32)[None, :]
    block_ids = jnp.arange(blocks, dtype=jnp.int32)[:, None, None]
    position = start + block_ids * WIN + cols_j[None] - WIN
    allowed = (cols_j > rows_i)[None] & (cols_j <= rows_i + WIN)[None] & (position >= 0)
    allowed = allowed[:, None]
    top = jnp.max(jnp.where(allowed, scores, jnp.float32(-1e30)), axis=-1, keepdims=True)
    prob = jnp.where(allowed, jnp.exp(scores - top), jnp.float32(0.0))
    total = jnp.sum(prob, axis=-1)
    out = jnp.einsum(
        "bhij,bjhe->bihe", prob.astype(jnp.bfloat16), vals, preferred_element_type=jnp.float32
    )
    out = out / jnp.transpose(total, (0, 2, 1))[..., None]
    return out.reshape(count, width)


def inner_causal(queries, keys, values):
    count = queries.shape[0]
    sim = jnp.einsum("thf,shf->hts", queries, keys, preferred_element_type=jnp.float32) * 0.25
    row_pos = jnp.arange(count, dtype=jnp.int32)
    causal = row_pos[:, None] >= row_pos[None, :]
    weights = jnp.where(causal[None], 1.0 + sim + 0.5 * sim * sim, jnp.float32(0.0))
    denom_parts = jnp.sum(weights, axis=-1)
    numer_parts = jnp.einsum(
        "hts,shv->htv", weights.astype(jnp.bfloat16), values, preferred_element_type=jnp.float32
    )
    return (numer_parts, denom_parts)


def head_sum(part, axis):
    size = lax.axis_size(axis)
    total = part
    step = 1
    while step < size:
        pairs = [(i, i ^ step) for i in range(size)]
        total = total + lax.ppermute(total, axis, pairs)
        step *= 2
    return total


def body(lin_query, lin_key, lin_values, win_query, win_key, win_value, conv_weight, head_gain):
    count = lin_query.shape[0]
    heads = lin_query.shape[1] // FDIM
    queries = lin_query.reshape(count, heads, FDIM)
    keys = lin_key.reshape(count, heads, FDIM)
    values = lin_values.reshape(count, heads, VDIM)
    values32 = values.astype(jnp.float32)
    phi_q = compact_features(queries, True)
    phi_k = compact_features(keys, False)
    feat = phi_k.shape[1]
    local_state = jnp.einsum("hft,thv->hfv", phi_k, values32, precision=HIGH)
    local_norm = jnp.sum(phi_k, axis=-1)
    size = lax.axis_size("cc") * 128
    packed = jnp.concatenate([local_state.reshape(-1), local_norm.reshape(-1)])
    used = packed.shape[0]
    quantum = size * 128
    padded = -(-used // quantum) * quantum
    packed = jnp.pad(packed, (0, padded - used))
    prior = exclusive_prefix(packed)
    split = heads * feat * VDIM
    prior_state = prior[:split].reshape(heads, feat, VDIM)
    prior_norm = prior[split:used].reshape(heads, feat)
    start = lax.axis_index(CTX) * count
    rims = passed_along((win_key[count - WIN :], win_value[count - WIN :]), CTX, 1)
    key_ext = jnp.concatenate([rims[0], win_key], axis=0)
    value_ext = jnp.concatenate([rims[1], win_value], axis=0)
    window_out = window_slab(win_query, key_ext, value_ext, start)
    taps = conv_weight.astype(jnp.float32)
    value_f32 = value_ext.astype(jnp.float32)
    conv_out = jnp.zeros((count, value_ext.shape[1]), jnp.float32)
    for tap in range(TAPS):
        conv_out = conv_out + taps[tap][None, :] * value_f32[WIN - tap : WIN - tap + count]
    inner_num, inner_den = inner_causal(queries, keys, values)
    numer = inner_num + jnp.einsum("hft,hfv->htv", phi_q, prior_state, precision=HIGH)
    denom = inner_den + jnp.einsum("hft,hf->ht", phi_q, prior_norm, precision=HIGH)
    lin_out = jnp.transpose(numer / denom[..., None], (1, 0, 2)).reshape(count, heads * VDIM)
    mixed = head_gain[None, :] * (lin_out + window_out + conv_out)
    squares = head_sum(jnp.sum(mixed * mixed, axis=-1), "head")
    msq = squares / D
    return (mixed * lax.rsqrt(msq + 1e-06)[:, None]).astype(jnp.bfloat16)


def split_ctx(mesh):
    column = mesh.devices[:, 0]
    xs = len({d.coords[0] for d in column})
    cores = len({d.core_on_chip for d in column})
    zs = column.shape[0] // (xs * cores)
    grid = mesh.devices.reshape(xs, zs, cores, mesh.devices.shape[1])
    return Mesh(grid, ("cx", "cz", "cc", "head"))


def solution(mesh):
    mesh = split_ctx(mesh)
    placed = (
        P(CTX, "head"),
        P(CTX, "head"),
        P(CTX, "head"),
        P(CTX, "head"),
        P(CTX, "head"),
        P(CTX, "head"),
        P(None, "head"),
        P("head"),
    )
    return jax.shard_map(
        body, mesh=mesh, in_specs=placed, out_specs=P(CTX, "head"), check_vma=False
    )
```

```python
import math

import numpy as np
import jax
import jax.numpy as jnp
from jax import lax
from jax.sharding import Mesh, PartitionSpec as P

FDIM = 16
VDIM = 128
WIN = 64
TAPS = 3
D = 2048
HIGH = lax.Precision.HIGHEST


CTX = ("cx", "cz", "cc")


def passed_along(shard, axis, by):
    length = math.prod(lax.axis_size(a) for a in axis)
    pairs = [(i, i + by) for i in range(length) if 0 <= i + by < length]
    return lax.ppermute(shard, axis, pairs)


def features_outer(x_tok):
    xt = jnp.transpose(x_tok.astype(jnp.float32), (1, 2, 0))
    heads, fdim, count = xt.shape
    ones = jnp.ones((heads, 1, count), jnp.float32)
    outer = (xt[:, :, None, :] * xt[:, None, :, :]).reshape(heads, fdim * fdim, count) * (
        1.0 / math.sqrt(32.0)
    )
    return jnp.concatenate([ones, xt * 0.5, outer], axis=1)


def fold_matrix(fdim, doubled):
    full = 1 + fdim + fdim * fdim
    pairs = [(i, j) for i in range(fdim) for j in range(i, fdim)]
    fold = np.zeros((1 + fdim + len(pairs), full), np.float32)
    for r in range(1 + fdim):
        fold[r, r] = 1.0
    for r, (i, j) in enumerate(pairs):
        fold[1 + fdim + r, 1 + fdim + i * fdim + j] = 1.0
        if doubled and i != j:
            fold[1 + fdim + r, 1 + fdim + j * fdim + i] = 1.0
    return jnp.asarray(fold)


def compact_features(x_tok, doubled):
    full = features_outer(x_tok)
    fold = fold_matrix(x_tok.shape[-1], doubled)
    return jnp.einsum("cf,hft->hct", fold, full, precision=HIGH)


def masked_rows(rows, upto):
    keep = jnp.arange(rows.shape[0], dtype=jnp.int32)[:, None] < upto
    return jnp.sum(jnp.where(keep, rows, jnp.float32(0.0)), axis=0)


def exclusive_prefix(flat):
    cores = lax.axis_size("cc")
    core = lax.axis_index("cc")
    chips = lax.axis_size("cx") * lax.axis_size("cz")
    pair = lax.all_gather(flat, "cc")
    below_core = masked_rows(pair, core)
    chip = jnp.sum(pair, axis=0)
    share = lax.dynamic_index_in_dim(chip.reshape(cores, -1), core, 0, False)
    recv = lax.all_to_all(share.reshape(chips, -1), ("cx", "cz"), 0, 0, tiled=True)
    lower = jnp.asarray(np.tril(np.ones((chips, chips), np.float32), -1))
    pref = jnp.dot(lower, recv, precision=HIGH, preferred_element_type=jnp.float32)
    back = lax.all_to_all(pref, ("cx", "cz"), 0, 0, tiled=True)
    shares = lax.all_gather(back.reshape(-1), "cc")
    return shares.reshape(-1) + below_core


def window_slab(query, key_ext, value_ext, start):
    count, width = query.shape
    heads = width // VDIM
    blocks = count // WIN
    qb = query.reshape(blocks, WIN, heads, VDIM)
    keys = jnp.concatenate(
        [
            key_ext[:count].reshape(blocks, WIN, heads, VDIM),
            key_ext[WIN:].reshape(blocks, WIN, heads, VDIM),
        ],
        axis=1,
    )
    vals = jnp.concatenate(
        [
            value_ext[:count].reshape(blocks, WIN, heads, VDIM),
            value_ext[WIN:].reshape(blocks, WIN, heads, VDIM),
        ],
        axis=1,
    )
    scores = jnp.einsum("bihe,bjhe->bhij", qb, keys, preferred_element_type=jnp.float32) * (
        1.0 / math.sqrt(VDIM)
    )
    rows_i = jnp.arange(WIN, dtype=jnp.int32)[:, None]
    cols_j = jnp.arange(2 * WIN, dtype=jnp.int32)[None, :]
    block_ids = jnp.arange(blocks, dtype=jnp.int32)[:, None, None]
    position = start + block_ids * WIN + cols_j[None] - WIN
    allowed = (cols_j > rows_i)[None] & (cols_j <= rows_i + WIN)[None] & (position >= 0)
    allowed = allowed[:, None]
    top = jnp.max(jnp.where(allowed, scores, jnp.float32(-1e30)), axis=-1, keepdims=True)
    prob = jnp.where(allowed, jnp.exp(scores - top), jnp.float32(0.0))
    total = jnp.sum(prob, axis=-1)
    out = jnp.einsum(
        "bhij,bjhe->bihe", prob.astype(jnp.bfloat16), vals, preferred_element_type=jnp.float32
    )
    out = out / jnp.transpose(total, (0, 2, 1))[..., None]
    return out.reshape(count, width)


def inner_causal(queries, keys, values):
    count = queries.shape[0]
    sim = jnp.einsum("thf,shf->hts", queries, keys, preferred_element_type=jnp.float32) * 0.25
    row_pos = jnp.arange(count, dtype=jnp.int32)
    causal = row_pos[:, None] >= row_pos[None, :]
    weights = jnp.where(causal[None], 1.0 + sim + 0.5 * sim * sim, jnp.float32(0.0))
    denom_parts = jnp.sum(weights, axis=-1)
    numer_parts = jnp.einsum(
        "hts,shv->htv", weights.astype(jnp.bfloat16), values, preferred_element_type=jnp.float32
    )
    return (numer_parts, denom_parts)


def head_sum(part, axis):
    size = lax.axis_size(axis)
    total = part
    step = 1
    while step < size:
        pairs = [(i, i ^ step) for i in range(size)]
        total = total + lax.ppermute(total, axis, pairs)
        step *= 2
    return total


def body(lin_query, lin_key, lin_values, win_query, win_key, win_value, conv_weight, head_gain):
    count = lin_query.shape[0]
    heads = lin_query.shape[1] // FDIM
    queries = lin_query.reshape(count, heads, FDIM)
    keys = lin_key.reshape(count, heads, FDIM)
    values = lin_values.reshape(count, heads, VDIM)
    values32 = values.astype(jnp.float32)
    phi_q = compact_features(queries, True)
    phi_k = compact_features(keys, False)
    feat = phi_k.shape[1]
    local_state = jnp.einsum("hft,thv->hfv", phi_k, values32, precision=HIGH)
    local_norm = jnp.sum(phi_k, axis=-1)
    size = lax.axis_size("cc") * lax.axis_size("cx") * lax.axis_size("cz")
    packed = jnp.concatenate([local_state.reshape(-1), local_norm.reshape(-1)])
    used = packed.shape[0]
    quantum = size * 128
    padded = -(-used // quantum) * quantum
    packed = jnp.pad(packed, (0, padded - used))
    prior = exclusive_prefix(packed)
    split = heads * feat * VDIM
    prior_state = prior[:split].reshape(heads, feat, VDIM)
    prior_norm = prior[split:used].reshape(heads, feat)
    start = lax.axis_index(CTX) * count
    rims = passed_along((win_key[count - WIN :], win_value[count - WIN :]), CTX, 1)
    key_ext = jnp.concatenate([rims[0], win_key], axis=0)
    value_ext = jnp.concatenate([rims[1], win_value], axis=0)
    window_out = window_slab(win_query, key_ext, value_ext, start)
    taps = conv_weight.astype(jnp.float32)
    value_f32 = value_ext.astype(jnp.float32)
    conv_out = jnp.zeros((count, value_ext.shape[1]), jnp.float32)
    for tap in range(TAPS):
        conv_out = conv_out + taps[tap][None, :] * value_f32[WIN - tap : WIN - tap + count]
    inner_num, inner_den = inner_causal(queries, keys, values)
    numer = inner_num + jnp.einsum("hft,hfv->htv", phi_q, prior_state, precision=HIGH)
    denom = inner_den + jnp.einsum("hft,hf->ht", phi_q, prior_norm, precision=HIGH)
    lin_out = jnp.transpose(numer / denom[..., None], (1, 0, 2)).reshape(count, heads * VDIM)
    mixed = head_gain[None, :] * (lin_out + window_out + conv_out)
    squares = head_sum(jnp.sum(mixed * mixed, axis=-1), "head")
    msq = squares / D
    return (mixed * lax.rsqrt(msq + 1e-06)[:, None]).astype(jnp.bfloat16)


def split_ctx(mesh):
    column = mesh.devices[:, 0]
    xs = len({d.coords[0] for d in column})
    cores = len({d.core_on_chip for d in column})
    zs = column.shape[0] // (xs * cores)
    grid = mesh.devices.reshape(xs, zs, cores, mesh.devices.shape[1])
    return Mesh(grid, ("cx", "cz", "cc", "head"))


def solution(mesh):
    mesh = split_ctx(mesh)
    placed = (
        P(CTX, "head"),
        P(CTX, "head"),
        P(CTX, "head"),
        P(CTX, "head"),
        P(CTX, "head"),
        P(CTX, "head"),
        P(None, "head"),
        P("head"),
    )
    return jax.shard_map(
        body, mesh=mesh, in_specs=placed, out_specs=P(CTX, "head"), check_vma=False
    )
```

```python
import math

import numpy as np
import jax
import jax.numpy as jnp
from jax import lax
from jax.sharding import Mesh, PartitionSpec as P

FDIM = 16
VDIM = 128
WIN = 64
TAPS = 3
D = 2048
HIGH = lax.Precision.HIGHEST


CTX = ("cx", "cz", "cc")


def passed_along(shard, axis, by):
    length = math.prod(lax.axis_size(a) for a in axis)
    pairs = [(i, i + by) for i in range(length) if 0 <= i + by < length]
    return lax.ppermute(shard, axis, pairs)


def features_outer(x_tok):
    xt = jnp.transpose(x_tok.astype(jnp.float32), (1, 2, 0))
    heads, fdim, count = xt.shape
    ones = jnp.ones((heads, 1, count), jnp.float32)
    outer = (xt[:, :, None, :] * xt[:, None, :, :]).reshape(heads, fdim * fdim, count) * (
        1.0 / math.sqrt(32.0)
    )
    return jnp.concatenate([ones, xt * 0.5, outer], axis=1)


def fold_matrix(fdim, doubled):
    full = 1 + fdim + fdim * fdim
    pairs = [(i, j) for i in range(fdim) for j in range(i, fdim)]
    fold = np.zeros((1 + fdim + len(pairs), full), np.float32)
    for r in range(1 + fdim):
        fold[r, r] = 1.0
    for r, (i, j) in enumerate(pairs):
        fold[1 + fdim + r, 1 + fdim + i * fdim + j] = 1.0
        if doubled and i != j:
            fold[1 + fdim + r, 1 + fdim + j * fdim + i] = 1.0
    return jnp.asarray(fold)


def compact_features(x_tok, doubled):
    full = features_outer(x_tok)
    fold = fold_matrix(x_tok.shape[-1], doubled)
    return jnp.einsum("cf,hft->hct", fold, full, precision=HIGH)


def masked_rows(rows, upto):
    keep = jnp.arange(rows.shape[0], dtype=jnp.int32)[:, None] < upto
    return jnp.sum(jnp.where(keep, rows, jnp.float32(0.0)), axis=0)


def exclusive_prefix(flat):
    cores = lax.axis_size("cc")
    core = lax.axis_index("cc")
    chips = lax.axis_size("cx") * lax.axis_size("cz")
    pair = lax.all_gather(flat, "cc")
    below_core = masked_rows(pair, core)
    chip = jnp.sum(pair, axis=0)
    share = lax.dynamic_index_in_dim(chip.reshape(cores, -1), core, 0, False)
    recv = lax.all_to_all(share.reshape(chips, -1), ("cx", "cz"), 0, 0, tiled=True)
    lower = jnp.asarray(np.tril(np.ones((chips, chips), np.float32), -1))
    pref = jnp.dot(lower, recv, precision=HIGH, preferred_element_type=jnp.float32)
    back = lax.all_to_all(pref, ("cx", "cz"), 0, 0, tiled=True)
    shares = lax.all_gather(back.reshape(-1), "cc")
    return shares.reshape(-1) + below_core


def window_slab(query, key_ext, value_ext, start):
    count, width = query.shape
    heads = width // VDIM
    blocks = count // WIN
    qb = query.reshape(blocks, WIN, heads, VDIM)
    keys = jnp.concatenate(
        [
            key_ext[:count].reshape(blocks, WIN, heads, VDIM),
            key_ext[WIN:].reshape(blocks, WIN, heads, VDIM),
        ],
        axis=1,
    )
    vals = jnp.concatenate(
        [
            value_ext[:count].reshape(blocks, WIN, heads, VDIM),
            value_ext[WIN:].reshape(blocks, WIN, heads, VDIM),
        ],
        axis=1,
    )
    scores = jnp.einsum("bihe,bjhe->bhij", qb, keys, preferred_element_type=jnp.float32) * (
        1.0 / math.sqrt(VDIM)
    )
    rows_i = jnp.arange(WIN, dtype=jnp.int32)[:, None]
    cols_j = jnp.arange(2 * WIN, dtype=jnp.int32)[None, :]
    block_ids = jnp.arange(blocks, dtype=jnp.int32)[:, None, None]
    position = start + block_ids * WIN + cols_j[None] - WIN
    allowed = (cols_j > rows_i)[None] & (cols_j <= rows_i + WIN)[None] & (position >= 0)
    allowed = allowed[:, None]
    top = jnp.max(jnp.where(allowed, scores, jnp.float32(-1e30)), axis=-1, keepdims=True)
    prob = jnp.where(allowed, jnp.exp(scores - top), jnp.float32(0.0))
    total = jnp.sum(prob, axis=-1)
    out = jnp.einsum(
        "bhij,bjhe->bihe", prob.astype(jnp.bfloat16), vals, preferred_element_type=jnp.float32
    )
    out = out / jnp.transpose(total, (0, 2, 1))[..., None]
    return out.reshape(count, width)


def inner_causal(queries, keys, values):
    count = queries.shape[0]
    sim = jnp.einsum("thf,shf->hts", queries, keys, preferred_element_type=jnp.float32) * 0.25
    row_pos = jnp.arange(count, dtype=jnp.int32)
    causal = row_pos[:, None] >= row_pos[None, :]
    weights = jnp.where(causal[None], 1.0 + sim + 0.5 * sim * sim, jnp.float32(0.0))
    denom_parts = jnp.sum(weights, axis=-1)
    numer_parts = jnp.einsum(
        "hts,shv->htv", weights.astype(jnp.bfloat16), values, preferred_element_type=jnp.float32
    )
    return (numer_parts, denom_parts)


def head_sum(part, axis):
    size = lax.axis_size(axis)
    total = part
    for step in range(1, size):
        pairs = [(i, (i + step) % size) for i in range(size)]
        total = total + lax.ppermute(part, axis, pairs)
    return total


def body(lin_query, lin_key, lin_values, win_query, win_key, win_value, conv_weight, head_gain):
    count = lin_query.shape[0]
    heads = lin_query.shape[1] // FDIM
    queries = lin_query.reshape(count, heads, FDIM)
    keys = lin_key.reshape(count, heads, FDIM)
    values = lin_values.reshape(count, heads, VDIM)
    values32 = values.astype(jnp.float32)
    phi_q = compact_features(queries, True)
    phi_k = compact_features(keys, False)
    feat = phi_k.shape[1]
    local_state = jnp.einsum("hft,thv->hfv", phi_k, values32, precision=HIGH)
    local_norm = jnp.sum(phi_k, axis=-1)
    size = lax.axis_size("cc") * lax.axis_size("cx") * lax.axis_size("cz")
    packed = jnp.concatenate([local_state.reshape(-1), local_norm.reshape(-1)])
    used = packed.shape[0]
    quantum = size * 128
    padded = -(-used // quantum) * quantum
    packed = jnp.pad(packed, (0, padded - used))
    prior = exclusive_prefix(packed)
    split = heads * feat * VDIM
    prior_state = prior[:split].reshape(heads, feat, VDIM)
    prior_norm = prior[split:used].reshape(heads, feat)
    start = lax.axis_index(CTX) * count
    rims = passed_along((win_key[count - WIN :], win_value[count - WIN :]), CTX, 1)
    key_ext = jnp.concatenate([rims[0], win_key], axis=0)
    value_ext = jnp.concatenate([rims[1], win_value], axis=0)
    window_out = window_slab(win_query, key_ext, value_ext, start)
    taps = conv_weight.astype(jnp.float32)
    value_f32 = value_ext.astype(jnp.float32)
    conv_out = jnp.zeros((count, value_ext.shape[1]), jnp.float32)
    for tap in range(TAPS):
        conv_out = conv_out + taps[tap][None, :] * value_f32[WIN - tap : WIN - tap + count]
    inner_num, inner_den = inner_causal(queries, keys, values)
    numer = inner_num + jnp.einsum("hft,hfv->htv", phi_q, prior_state, precision=HIGH)
    denom = inner_den + jnp.einsum("hft,hf->ht", phi_q, prior_norm, precision=HIGH)
    lin_out = jnp.transpose(numer / denom[..., None], (1, 0, 2)).reshape(count, heads * VDIM)
    mixed = head_gain[None, :] * (lin_out + window_out + conv_out)
    squares = head_sum(jnp.sum(mixed * mixed, axis=-1), "head")
    msq = squares / D
    return (mixed * lax.rsqrt(msq + 1e-06)[:, None]).astype(jnp.bfloat16)


def split_ctx(mesh):
    column = mesh.devices[:, 0]
    xs = len({d.coords[0] for d in column})
    cores = len({d.core_on_chip for d in column})
    zs = column.shape[0] // (xs * cores)
    grid = mesh.devices.reshape(xs, zs, cores, mesh.devices.shape[1])
    return Mesh(grid, ("cx", "cz", "cc", "head"))


def solution(mesh):
    mesh = split_ctx(mesh)
    placed = (
        P(CTX, "head"),
        P(CTX, "head"),
        P(CTX, "head"),
        P(CTX, "head"),
        P(CTX, "head"),
        P(CTX, "head"),
        P(None, "head"),
        P("head"),
    )
    return jax.shard_map(
        body, mesh=mesh, in_specs=placed, out_specs=P(CTX, "head"), check_vma=False
    )
```

```python
import math

import numpy as np
import jax
import jax.numpy as jnp
from jax import lax
from jax.sharding import Mesh, PartitionSpec as P

FDIM = 16
VDIM = 128
WIN = 64
TAPS = 3
D = 2048
HIGH = lax.Precision.HIGHEST


CTX = ("cx", "cz", "cc")


def passed_along(shard, axis, by):
    length = math.prod(lax.axis_size(a) for a in axis)
    pairs = [(i, i + by) for i in range(length) if 0 <= i + by < length]
    return lax.ppermute(shard, axis, pairs)


def features_outer(x_tok):
    xt = jnp.transpose(x_tok.astype(jnp.float32), (1, 2, 0))
    heads, fdim, count = xt.shape
    ones = jnp.ones((heads, 1, count), jnp.float32)
    outer = (xt[:, :, None, :] * xt[:, None, :, :]).reshape(heads, fdim * fdim, count) * (
        1.0 / math.sqrt(32.0)
    )
    return jnp.concatenate([ones, xt * 0.5, outer], axis=1)


def fold_matrix(fdim, doubled):
    full = 1 + fdim + fdim * fdim
    pairs = [(i, j) for i in range(fdim) for j in range(i, fdim)]
    fold = np.zeros((1 + fdim + len(pairs), full), np.float32)
    for r in range(1 + fdim):
        fold[r, r] = 1.0
    for r, (i, j) in enumerate(pairs):
        fold[1 + fdim + r, 1 + fdim + i * fdim + j] = 1.0
        if doubled and i != j:
            fold[1 + fdim + r, 1 + fdim + j * fdim + i] = 1.0
    return jnp.asarray(fold)


def compact_features(x_tok, doubled):
    full = features_outer(x_tok)
    fold = fold_matrix(x_tok.shape[-1], doubled)
    return jnp.einsum("cf,hft->hct", fold, full, precision=HIGH)


def masked_rows(rows, upto):
    keep = jnp.arange(rows.shape[0], dtype=jnp.int32)[:, None] < upto
    return jnp.sum(jnp.where(keep, rows, jnp.float32(0.0)), axis=0)


def exclusive_prefix(flat):
    cores = lax.axis_size("cc")
    core = lax.axis_index("cc")
    chips = lax.axis_size("cx") * lax.axis_size("cz")
    pair = lax.all_gather(flat, "cc")
    below_core = masked_rows(pair, core)
    chip = jnp.sum(pair, axis=0)
    share = lax.dynamic_index_in_dim(chip.reshape(cores, -1), core, 0, False)
    recv = lax.all_to_all(share.reshape(chips, -1), ("cx", "cz"), 0, 0, tiled=True)
    lower = jnp.asarray(np.tril(np.ones((chips, chips), np.float32), -1))
    pref = jnp.dot(lower, recv, precision=HIGH, preferred_element_type=jnp.float32)
    back = lax.all_to_all(pref, ("cx", "cz"), 0, 0, tiled=True)
    shares = lax.all_gather(back.reshape(-1), "cc")
    return shares.reshape(-1) + below_core


def window_slab(query, key_ext, value_ext, start):
    count, width = query.shape
    heads = width // VDIM
    blocks = count // WIN
    qb = query.reshape(blocks, WIN, heads, VDIM)
    keys = jnp.concatenate(
        [
            key_ext[:count].reshape(blocks, WIN, heads, VDIM),
            key_ext[WIN:].reshape(blocks, WIN, heads, VDIM),
        ],
        axis=1,
    )
    vals = jnp.concatenate(
        [
            value_ext[:count].reshape(blocks, WIN, heads, VDIM),
            value_ext[WIN:].reshape(blocks, WIN, heads, VDIM),
        ],
        axis=1,
    )
    scores = jnp.einsum("bihe,bjhe->bhij", qb, keys, preferred_element_type=jnp.float32) * (
        1.0 / math.sqrt(VDIM)
    )
    rows_i = jnp.arange(WIN, dtype=jnp.int32)[:, None]
    cols_j = jnp.arange(2 * WIN, dtype=jnp.int32)[None, :]
    block_ids = jnp.arange(blocks, dtype=jnp.int32)[:, None, None]
    position = start + block_ids * WIN + cols_j[None] - WIN
    allowed = (cols_j > rows_i)[None] & (cols_j <= rows_i + WIN)[None] & (position >= 0)
    allowed = allowed[:, None]
    top = jnp.max(jnp.where(allowed, scores, jnp.float32(-1e30)), axis=-1, keepdims=True)
    prob = jnp.where(allowed, jnp.exp(scores - top), jnp.float32(0.0))
    total = jnp.sum(prob, axis=-1)
    out = jnp.einsum(
        "bhij,bjhe->bihe", prob.astype(jnp.bfloat16), vals, preferred_element_type=jnp.float32
    )
    out = out / jnp.transpose(total, (0, 2, 1))[..., None]
    return out.reshape(count, width)


def inner_causal(queries, keys, values):
    count = queries.shape[0]
    sim = jnp.einsum("thf,shf->hts", queries, keys, preferred_element_type=jnp.float32) * 0.25
    row_pos = jnp.arange(count, dtype=jnp.int32)
    causal = row_pos[:, None] >= row_pos[None, :]
    weights = jnp.where(causal[None], 1.0 + sim + 0.5 * sim * sim, jnp.float32(0.0))
    denom_parts = jnp.sum(weights, axis=-1)
    numer_parts = jnp.einsum(
        "hts,shv->htv", weights.astype(jnp.bfloat16), values, preferred_element_type=jnp.float32
    )
    return (numer_parts, denom_parts)


def head_sum(part, axis):
    size = lax.axis_size(axis)
    total = part
    step = 1
    while step < size:
        pairs = [(i, i ^ step) for i in range(size)]
        total = total + lax.ppermute(total, axis, pairs)
        step *= 2
    return total


def body(lin_query, lin_key, lin_values, win_query, win_key, win_value, conv_weight, head_gain):
    count = lin_query.shape[0]
    heads = lin_query.shape[1] // FDIM
    queries = lin_query.reshape(count, heads, FDIM)
    keys = lin_key.reshape(count, heads, FDIM)
    values = lin_values.reshape(count, heads, VDIM)
    values32 = values.astype(jnp.float32)
    phi_q = compact_features(queries, True)
    phi_k = compact_features(keys, False)
    feat = phi_k.shape[1]
    local_state = jnp.einsum("hft,thv->hfv", phi_k, values32, precision=HIGH)
    local_norm = jnp.sum(phi_k, axis=-1)
    size = lax.axis_size("cc") * lax.axis_size("cx") * lax.axis_size("cz")
    packed = jnp.concatenate([local_state.reshape(-1), local_norm.reshape(-1)])
    used = packed.shape[0]
    quantum = size * 128
    padded = -(-used // quantum) * quantum
    packed = jnp.pad(packed, (0, padded - used))
    prior = exclusive_prefix(packed)
    split = heads * feat * VDIM
    prior_state = prior[:split].reshape(heads, feat, VDIM)
    prior_norm = prior[split:used].reshape(heads, feat)
    start = lax.axis_index(CTX) * count
    rims = passed_along((win_key[count - WIN :], win_value[count - WIN :]), CTX, 1)
    key_ext = jnp.concatenate([rims[0], win_key], axis=0)
    value_ext = jnp.concatenate([rims[1], win_value], axis=0)
    window_out = window_slab(win_query, key_ext, value_ext, start)
    taps = conv_weight.astype(jnp.float32)
    value_f32 = value_ext.astype(jnp.float32)
    conv_out = jnp.zeros((count, value_ext.shape[1]), jnp.float32)
    for tap in range(TAPS):
        conv_out = conv_out + taps[tap][None, :] * value_f32[WIN - tap : WIN - tap + count]
    inner_num, inner_den = inner_causal(queries, keys, values)
    numer = inner_num + jnp.einsum("hft,hfv->htv", phi_q, prior_state, precision=HIGH)
    denom = inner_den + jnp.einsum("hft,hf->ht", phi_q, prior_norm, precision=HIGH)
    lin_out = jnp.transpose(numer / denom[..., None], (1, 0, 2)).reshape(count, heads * VDIM)
    mixed = head_gain[None, :] * (lin_out + window_out + conv_out)
    squares = jnp.sum(lax.all_gather(jnp.sum(mixed * mixed, axis=-1), "head"), axis=0)
    msq = squares / D
    return (mixed * lax.rsqrt(msq + 1e-06)[:, None]).astype(jnp.bfloat16)


def split_ctx(mesh):
    column = mesh.devices[:, 0]
    xs = len({d.coords[0] for d in column})
    cores = len({d.core_on_chip for d in column})
    zs = column.shape[0] // (xs * cores)
    grid = mesh.devices.reshape(xs, zs, cores, mesh.devices.shape[1])
    return Mesh(grid, ("cx", "cz", "cc", "head"))


def solution(mesh):
    mesh = split_ctx(mesh)
    placed = (
        P(CTX, "head"),
        P(CTX, "head"),
        P(CTX, "head"),
        P(CTX, "head"),
        P(CTX, "head"),
        P(CTX, "head"),
        P(None, "head"),
        P("head"),
    )
    return jax.shard_map(
        body, mesh=mesh, in_specs=placed, out_specs=P(CTX, "head"), check_vma=False
    )
```

```python
import math

import numpy as np
import jax
import jax.numpy as jnp
from jax import lax
from jax.sharding import Mesh, PartitionSpec as P

FDIM = 16
VDIM = 128
WIN = 64
TAPS = 3
D = 2048
HIGH = lax.Precision.HIGHEST
THREE = lax.Precision.HIGH


CTX = ("cx", "cz", "cc")


def passed_along(shard, axis, by):
    length = math.prod(lax.axis_size(a) for a in axis)
    pairs = [(i, i + by) for i in range(length) if 0 <= i + by < length]
    return lax.ppermute(shard, axis, pairs)


def features_outer(x_tok):
    xt = jnp.transpose(x_tok.astype(jnp.float32), (1, 2, 0))
    heads, fdim, count = xt.shape
    ones = jnp.ones((heads, 1, count), jnp.float32)
    outer = (xt[:, :, None, :] * xt[:, None, :, :]).reshape(heads, fdim * fdim, count) * (
        1.0 / math.sqrt(32.0)
    )
    return jnp.concatenate([ones, xt * 0.5, outer], axis=1)


def fold_matrix(fdim, doubled):
    full = 1 + fdim + fdim * fdim
    pairs = [(i, j) for i in range(fdim) for j in range(i, fdim)]
    fold = np.zeros((1 + fdim + len(pairs), full), np.float32)
    for r in range(1 + fdim):
        fold[r, r] = 1.0
    for r, (i, j) in enumerate(pairs):
        fold[1 + fdim + r, 1 + fdim + i * fdim + j] = 1.0
        if doubled and i != j:
            fold[1 + fdim + r, 1 + fdim + j * fdim + i] = 1.0
    return jnp.asarray(fold)


def compact_features(x_tok, doubled):
    full = features_outer(x_tok)
    fold = fold_matrix(x_tok.shape[-1], doubled)
    return jnp.einsum("cf,hft->hct", fold, full, precision=THREE)


def masked_rows(rows, upto):
    keep = jnp.arange(rows.shape[0], dtype=jnp.int32)[:, None] < upto
    return jnp.sum(jnp.where(keep, rows, jnp.float32(0.0)), axis=0)


def exclusive_prefix(flat):
    cores = lax.axis_size("cc")
    core = lax.axis_index("cc")
    chips = lax.axis_size("cx") * lax.axis_size("cz")
    pair = lax.all_gather(flat, "cc")
    below_core = masked_rows(pair, core)
    chip = jnp.sum(pair, axis=0)
    share = lax.dynamic_index_in_dim(chip.reshape(cores, -1), core, 0, False)
    recv = lax.all_to_all(share.reshape(chips, -1), ("cx", "cz"), 0, 0, tiled=True)
    lower = jnp.asarray(np.tril(np.ones((chips, chips), np.float32), -1))
    pref = jnp.dot(lower, recv, precision=HIGH, preferred_element_type=jnp.float32)
    back = lax.all_to_all(pref, ("cx", "cz"), 0, 0, tiled=True)
    shares = lax.all_gather(back.reshape(-1), "cc")
    return shares.reshape(-1) + below_core


def window_slab(query, key_ext, value_ext, start):
    count, width = query.shape
    heads = width // VDIM
    blocks = count // WIN
    qb = query.reshape(blocks, WIN, heads, VDIM)
    keys = jnp.concatenate(
        [
            key_ext[:count].reshape(blocks, WIN, heads, VDIM),
            key_ext[WIN:].reshape(blocks, WIN, heads, VDIM),
        ],
        axis=1,
    )
    vals = jnp.concatenate(
        [
            value_ext[:count].reshape(blocks, WIN, heads, VDIM),
            value_ext[WIN:].reshape(blocks, WIN, heads, VDIM),
        ],
        axis=1,
    )
    scores = jnp.einsum("bihe,bjhe->bhij", qb, keys, preferred_element_type=jnp.float32) * (
        1.0 / math.sqrt(VDIM)
    )
    rows_i = jnp.arange(WIN, dtype=jnp.int32)[:, None]
    cols_j = jnp.arange(2 * WIN, dtype=jnp.int32)[None, :]
    block_ids = jnp.arange(blocks, dtype=jnp.int32)[:, None, None]
    position = start + block_ids * WIN + cols_j[None] - WIN
    allowed = (cols_j > rows_i)[None] & (cols_j <= rows_i + WIN)[None] & (position >= 0)
    allowed = allowed[:, None]
    top = jnp.max(jnp.where(allowed, scores, jnp.float32(-1e30)), axis=-1, keepdims=True)
    prob = jnp.where(allowed, jnp.exp(scores - top), jnp.float32(0.0))
    total = jnp.sum(prob, axis=-1)
    out = jnp.einsum(
        "bhij,bjhe->bihe", prob.astype(jnp.bfloat16), vals, preferred_element_type=jnp.float32
    )
    out = out / jnp.transpose(total, (0, 2, 1))[..., None]
    return out.reshape(count, width)


def inner_causal(queries, keys, values):
    count = queries.shape[0]
    sim = jnp.einsum("thf,shf->hts", queries, keys, preferred_element_type=jnp.float32) * 0.25
    row_pos = jnp.arange(count, dtype=jnp.int32)
    causal = row_pos[:, None] >= row_pos[None, :]
    weights = jnp.where(causal[None], 1.0 + sim + 0.5 * sim * sim, jnp.float32(0.0))
    denom_parts = jnp.sum(weights, axis=-1)
    numer_parts = jnp.einsum(
        "hts,shv->htv", weights.astype(jnp.bfloat16), values, preferred_element_type=jnp.float32
    )
    return (numer_parts, denom_parts)


def head_sum(part, axis):
    size = lax.axis_size(axis)
    total = part
    step = 1
    while step < size:
        pairs = [(i, i ^ step) for i in range(size)]
        total = total + lax.ppermute(total, axis, pairs)
        step *= 2
    return total


def body(lin_query, lin_key, lin_values, win_query, win_key, win_value, conv_weight, head_gain):
    count = lin_query.shape[0]
    heads = lin_query.shape[1] // FDIM
    queries = lin_query.reshape(count, heads, FDIM)
    keys = lin_key.reshape(count, heads, FDIM)
    values = lin_values.reshape(count, heads, VDIM)
    values32 = values.astype(jnp.float32)
    phi_q = compact_features(queries, True)
    phi_k = compact_features(keys, False)
    feat = phi_k.shape[1]
    local_state = jnp.einsum("hft,thv->hfv", phi_k, values32, precision=THREE)
    local_norm = jnp.sum(phi_k, axis=-1)
    size = lax.axis_size("cc") * lax.axis_size("cx") * lax.axis_size("cz")
    packed = jnp.concatenate([local_state.reshape(-1), local_norm.reshape(-1)])
    used = packed.shape[0]
    quantum = size * 128
    padded = -(-used // quantum) * quantum
    packed = jnp.pad(packed, (0, padded - used))
    prior = exclusive_prefix(packed)
    split = heads * feat * VDIM
    prior_state = prior[:split].reshape(heads, feat, VDIM)
    prior_norm = prior[split:used].reshape(heads, feat)
    start = lax.axis_index(CTX) * count
    rims = passed_along((win_key[count - WIN :], win_value[count - WIN :]), CTX, 1)
    key_ext = jnp.concatenate([rims[0], win_key], axis=0)
    value_ext = jnp.concatenate([rims[1], win_value], axis=0)
    window_out = window_slab(win_query, key_ext, value_ext, start)
    taps = conv_weight.astype(jnp.float32)
    value_f32 = value_ext.astype(jnp.float32)
    conv_out = jnp.zeros((count, value_ext.shape[1]), jnp.float32)
    for tap in range(TAPS):
        conv_out = conv_out + taps[tap][None, :] * value_f32[WIN - tap : WIN - tap + count]
    inner_num, inner_den = inner_causal(queries, keys, values)
    numer = inner_num + jnp.einsum("hft,hfv->htv", phi_q, prior_state, precision=THREE)
    denom = inner_den + jnp.einsum("hft,hf->ht", phi_q, prior_norm, precision=THREE)
    lin_out = jnp.transpose(numer / denom[..., None], (1, 0, 2)).reshape(count, heads * VDIM)
    mixed = head_gain[None, :] * (lin_out + window_out + conv_out)
    squares = jnp.sum(lax.all_gather(jnp.sum(mixed * mixed, axis=-1), "head"), axis=0)
    msq = squares / D
    return (mixed * lax.rsqrt(msq + 1e-06)[:, None]).astype(jnp.bfloat16)


def split_ctx(mesh):
    column = mesh.devices[:, 0]
    xs = len({d.coords[0] for d in column})
    cores = len({d.core_on_chip for d in column})
    zs = column.shape[0] // (xs * cores)
    grid = mesh.devices.reshape(xs, zs, cores, mesh.devices.shape[1])
    return Mesh(grid, ("cx", "cz", "cc", "head"))


def solution(mesh):
    mesh = split_ctx(mesh)
    placed = (
        P(CTX, "head"),
        P(CTX, "head"),
        P(CTX, "head"),
        P(CTX, "head"),
        P(CTX, "head"),
        P(CTX, "head"),
        P(None, "head"),
        P("head"),
    )
    return jax.shard_map(
        body, mesh=mesh, in_specs=placed, out_specs=P(CTX, "head"), check_vma=False
    )
```

```python
import math

import numpy as np
import jax
import jax.numpy as jnp
from jax import lax
from jax.sharding import Mesh, PartitionSpec as P

FDIM = 16
VDIM = 128
WIN = 64
TAPS = 3
D = 2048
HIGH = lax.Precision.HIGHEST
THREE = lax.Precision.HIGH


CTX = ("cx", "cz", "cc")


def passed_along(shard, axis, by):
    length = math.prod(lax.axis_size(a) for a in axis)
    pairs = [(i, i + by) for i in range(length) if 0 <= i + by < length]
    return lax.ppermute(shard, axis, pairs)


def features_outer(x_tok):
    xt = jnp.transpose(x_tok.astype(jnp.float32), (1, 2, 0))
    heads, fdim, count = xt.shape
    ones = jnp.ones((heads, 1, count), jnp.float32)
    outer = (xt[:, :, None, :] * xt[:, None, :, :]).reshape(heads, fdim * fdim, count) * (
        1.0 / math.sqrt(32.0)
    )
    return jnp.concatenate([ones, xt * 0.5, outer], axis=1)


def fold_matrix(fdim, doubled):
    full = 1 + fdim + fdim * fdim
    pairs = [(i, j) for i in range(fdim) for j in range(i, fdim)]
    fold = np.zeros((1 + fdim + len(pairs), full), np.float32)
    for r in range(1 + fdim):
        fold[r, r] = 1.0
    for r, (i, j) in enumerate(pairs):
        fold[1 + fdim + r, 1 + fdim + i * fdim + j] = 1.0
        if doubled and i != j:
            fold[1 + fdim + r, 1 + fdim + j * fdim + i] = 1.0
    return jnp.asarray(fold)


def compact_features(x_tok, doubled):
    full = features_outer(x_tok)
    fold = fold_matrix(x_tok.shape[-1], doubled)
    return jnp.einsum("cf,hft->hct", fold, full, precision=THREE)


def masked_rows(rows, upto):
    keep = jnp.arange(rows.shape[0], dtype=jnp.int32)[:, None] < upto
    return jnp.sum(jnp.where(keep, rows, jnp.float32(0.0)), axis=0)


def exclusive_prefix(flat):
    cores = lax.axis_size("cc")
    core = lax.axis_index("cc")
    chips = lax.axis_size("cx") * lax.axis_size("cz")
    pair = lax.all_gather(flat, "cc")
    below_core = masked_rows(pair, core)
    halves = pair.reshape(cores, cores, -1)
    share = jnp.sum(lax.dynamic_index_in_dim(halves, core, 1, False), axis=0)
    recv = lax.all_to_all(share.reshape(chips, -1), ("cx", "cz"), 0, 0, tiled=True)
    lower = jnp.asarray(np.tril(np.ones((chips, chips), np.float32), -1))
    pref = jnp.dot(lower, recv, precision=HIGH, preferred_element_type=jnp.float32)
    back = lax.all_to_all(pref, ("cx", "cz"), 0, 0, tiled=True)
    shares = lax.all_gather(back.reshape(-1), "cc")
    return shares.reshape(-1) + below_core


def window_slab(query, key_ext, value_ext, start):
    count, width = query.shape
    heads = width // VDIM
    blocks = count // WIN
    qb = query.reshape(blocks, WIN, heads, VDIM)
    keys = jnp.concatenate(
        [
            key_ext[:count].reshape(blocks, WIN, heads, VDIM),
            key_ext[WIN:].reshape(blocks, WIN, heads, VDIM),
        ],
        axis=1,
    )
    vals = jnp.concatenate(
        [
            value_ext[:count].reshape(blocks, WIN, heads, VDIM),
            value_ext[WIN:].reshape(blocks, WIN, heads, VDIM),
        ],
        axis=1,
    )
    scores = jnp.einsum("bihe,bjhe->bhij", qb, keys, preferred_element_type=jnp.float32) * (
        1.0 / math.sqrt(VDIM)
    )
    rows_i = jnp.arange(WIN, dtype=jnp.int32)[:, None]
    cols_j = jnp.arange(2 * WIN, dtype=jnp.int32)[None, :]
    block_ids = jnp.arange(blocks, dtype=jnp.int32)[:, None, None]
    position = start + block_ids * WIN + cols_j[None] - WIN
    allowed = (cols_j > rows_i)[None] & (cols_j <= rows_i + WIN)[None] & (position >= 0)
    allowed = allowed[:, None]
    top = jnp.max(jnp.where(allowed, scores, jnp.float32(-1e30)), axis=-1, keepdims=True)
    prob = jnp.where(allowed, jnp.exp(scores - top), jnp.float32(0.0))
    total = jnp.sum(prob, axis=-1)
    out = jnp.einsum(
        "bhij,bjhe->bihe", prob.astype(jnp.bfloat16), vals, preferred_element_type=jnp.float32
    )
    out = out / jnp.transpose(total, (0, 2, 1))[..., None]
    return out.reshape(count, width)


def inner_causal(queries, keys, values):
    count = queries.shape[0]
    sim = jnp.einsum("thf,shf->hts", queries, keys, preferred_element_type=jnp.float32) * 0.25
    row_pos = jnp.arange(count, dtype=jnp.int32)
    causal = row_pos[:, None] >= row_pos[None, :]
    weights = jnp.where(causal[None], 1.0 + sim + 0.5 * sim * sim, jnp.float32(0.0))
    denom_parts = jnp.sum(weights, axis=-1)
    numer_parts = jnp.einsum(
        "hts,shv->htv", weights.astype(jnp.bfloat16), values, preferred_element_type=jnp.float32
    )
    return (numer_parts, denom_parts)


def head_sum(part, axis):
    size = lax.axis_size(axis)
    total = part
    step = 1
    while step < size:
        pairs = [(i, i ^ step) for i in range(size)]
        total = total + lax.ppermute(total, axis, pairs)
        step *= 2
    return total


def body(lin_query, lin_key, lin_values, win_query, win_key, win_value, conv_weight, head_gain):
    count = lin_query.shape[0]
    heads = lin_query.shape[1] // FDIM
    queries = lin_query.reshape(count, heads, FDIM)
    keys = lin_key.reshape(count, heads, FDIM)
    values = lin_values.reshape(count, heads, VDIM)
    values32 = values.astype(jnp.float32)
    phi_q = compact_features(queries, True)
    phi_k = compact_features(keys, False)
    feat = phi_k.shape[1]
    local_state = jnp.einsum("hft,thv->hfv", phi_k, values32, precision=THREE)
    local_norm = jnp.sum(phi_k, axis=-1)
    size = lax.axis_size("cc") * lax.axis_size("cx") * lax.axis_size("cz")
    packed = jnp.concatenate([local_state.reshape(-1), local_norm.reshape(-1)])
    used = packed.shape[0]
    quantum = size * 128
    padded = -(-used // quantum) * quantum
    packed = jnp.pad(packed, (0, padded - used))
    prior = exclusive_prefix(packed)
    split = heads * feat * VDIM
    prior_state = prior[:split].reshape(heads, feat, VDIM)
    prior_norm = prior[split:used].reshape(heads, feat)
    start = lax.axis_index(CTX) * count
    rims = passed_along((win_key[count - WIN :], win_value[count - WIN :]), CTX, 1)
    key_ext = jnp.concatenate([rims[0], win_key], axis=0)
    value_ext = jnp.concatenate([rims[1], win_value], axis=0)
    window_out = window_slab(win_query, key_ext, value_ext, start)
    taps = conv_weight.astype(jnp.float32)
    value_f32 = value_ext.astype(jnp.float32)
    conv_out = jnp.zeros((count, value_ext.shape[1]), jnp.float32)
    for tap in range(TAPS):
        conv_out = conv_out + taps[tap][None, :] * value_f32[WIN - tap : WIN - tap + count]
    inner_num, inner_den = inner_causal(queries, keys, values)
    numer = inner_num + jnp.einsum("hft,hfv->htv", phi_q, prior_state, precision=THREE)
    denom = inner_den + jnp.einsum("hft,hf->ht", phi_q, prior_norm, precision=THREE)
    lin_out = jnp.transpose(numer / denom[..., None], (1, 0, 2)).reshape(count, heads * VDIM)
    mixed = head_gain[None, :] * (lin_out + window_out + conv_out)
    squares = jnp.sum(lax.all_gather(jnp.sum(mixed * mixed, axis=-1), "head"), axis=0)
    msq = squares / D
    return (mixed * lax.rsqrt(msq + 1e-06)[:, None]).astype(jnp.bfloat16)


def split_ctx(mesh):
    column = mesh.devices[:, 0]
    xs = len({d.coords[0] for d in column})
    cores = len({d.core_on_chip for d in column})
    zs = column.shape[0] // (xs * cores)
    grid = mesh.devices.reshape(xs, zs, cores, mesh.devices.shape[1])
    return Mesh(grid, ("cx", "cz", "cc", "head"))


def solution(mesh):
    mesh = split_ctx(mesh)
    placed = (
        P(CTX, "head"),
        P(CTX, "head"),
        P(CTX, "head"),
        P(CTX, "head"),
        P(CTX, "head"),
        P(CTX, "head"),
        P(None, "head"),
        P("head"),
    )
    return jax.shard_map(
        body, mesh=mesh, in_specs=placed, out_specs=P(CTX, "head"), check_vma=False
    )
```

```python
import math

import numpy as np
import jax
import jax.numpy as jnp
from jax import lax
from jax.sharding import Mesh, PartitionSpec as P

FDIM = 16
VDIM = 128
WIN = 64
TAPS = 3
D = 2048
HIGH = lax.Precision.HIGHEST
THREE = lax.Precision.HIGH


CTX = ("cx", "cz", "cc")


def passed_along(shard, axis, by):
    length = math.prod(lax.axis_size(a) for a in axis)
    pairs = [(i, i + by) for i in range(length) if 0 <= i + by < length]
    return lax.ppermute(shard, axis, pairs)


def pair_selectors(fdim, doubled):
    pairs = [(i, j) for i in range(fdim) for j in range(i, fdim)]
    left = np.zeros((len(pairs), fdim), np.float32)
    right = np.zeros((len(pairs), fdim), np.float32)
    for r, (i, j) in enumerate(pairs):
        left[r, i] = 2.0 if (doubled and i != j) else 1.0
        right[r, j] = 1.0
    return jnp.asarray(left, jnp.bfloat16), jnp.asarray(right, jnp.bfloat16)


def compact_features(x_tok, doubled):
    count, heads, fdim = x_tok.shape
    left, right = pair_selectors(fdim, doubled)
    xb = jnp.transpose(x_tok, (1, 2, 0))
    a = jnp.einsum("rf,hft->hrt", left, xb, preferred_element_type=jnp.float32)
    b = jnp.einsum("rf,hft->hrt", right, xb, preferred_element_type=jnp.float32)
    xt = xb.astype(jnp.float32)
    ones = jnp.ones((heads, 1, count), jnp.float32)
    outer = (a * b) * (1.0 / math.sqrt(32.0))
    return jnp.concatenate([ones, xt * 0.5, outer], axis=1)


def split_dot(feats, values):
    hi = feats.astype(jnp.bfloat16)
    lo = (feats - hi.astype(jnp.float32)).astype(jnp.bfloat16)
    first = jnp.einsum("hft,thv->hfv", hi, values, preferred_element_type=jnp.float32)
    second = jnp.einsum("hft,thv->hfv", lo, values, preferred_element_type=jnp.float32)
    return first + second


def masked_rows(rows, upto):
    keep = jnp.arange(rows.shape[0], dtype=jnp.int32)[:, None] < upto
    return jnp.sum(jnp.where(keep, rows, jnp.float32(0.0)), axis=0)


def exclusive_prefix(flat):
    cores = lax.axis_size("cc")
    core = lax.axis_index("cc")
    chips = lax.axis_size("cx") * lax.axis_size("cz")
    pair = lax.all_gather(flat, "cc")
    below_core = masked_rows(pair, core)
    halves = pair.reshape(cores, cores, -1)
    share = jnp.sum(lax.dynamic_index_in_dim(halves, core, 1, False), axis=0)
    recv = lax.all_to_all(share.reshape(chips, -1), ("cx", "cz"), 0, 0, tiled=True)
    lower = jnp.asarray(np.tril(np.ones((chips, chips), np.float32), -1))
    pref = jnp.dot(lower, recv, precision=HIGH, preferred_element_type=jnp.float32)
    back = lax.all_to_all(pref, ("cx", "cz"), 0, 0, tiled=True)
    shares = lax.all_gather(back.reshape(-1), "cc")
    return shares.reshape(-1) + below_core


def window_slab(query, key_ext, value_ext, start):
    count, width = query.shape
    heads = width // VDIM
    blocks = count // WIN
    qb = query.reshape(blocks, WIN, heads, VDIM)
    keys = jnp.concatenate(
        [
            key_ext[:count].reshape(blocks, WIN, heads, VDIM),
            key_ext[WIN:].reshape(blocks, WIN, heads, VDIM),
        ],
        axis=1,
    )
    vals = jnp.concatenate(
        [
            value_ext[:count].reshape(blocks, WIN, heads, VDIM),
            value_ext[WIN:].reshape(blocks, WIN, heads, VDIM),
        ],
        axis=1,
    )
    scores = jnp.einsum("bihe,bjhe->bhij", qb, keys, preferred_element_type=jnp.float32) * (
        1.0 / math.sqrt(VDIM)
    )
    rows_i = jnp.arange(WIN, dtype=jnp.int32)[:, None]
    cols_j = jnp.arange(2 * WIN, dtype=jnp.int32)[None, :]
    block_ids = jnp.arange(blocks, dtype=jnp.int32)[:, None, None]
    position = start + block_ids * WIN + cols_j[None] - WIN
    allowed = (cols_j > rows_i)[None] & (cols_j <= rows_i + WIN)[None] & (position >= 0)
    allowed = allowed[:, None]
    top = jnp.max(jnp.where(allowed, scores, jnp.float32(-1e30)), axis=-1, keepdims=True)
    prob = jnp.where(allowed, jnp.exp(scores - top), jnp.float32(0.0))
    total = jnp.sum(prob, axis=-1)
    out = jnp.einsum(
        "bhij,bjhe->bihe", prob.astype(jnp.bfloat16), vals, preferred_element_type=jnp.float32
    )
    out = out / jnp.transpose(total, (0, 2, 1))[..., None]
    return out.reshape(count, width)


def inner_causal(queries, keys, values):
    count = queries.shape[0]
    sim = jnp.einsum("thf,shf->hts", queries, keys, preferred_element_type=jnp.float32) * 0.25
    row_pos = jnp.arange(count, dtype=jnp.int32)
    causal = row_pos[:, None] >= row_pos[None, :]
    weights = jnp.where(causal[None], 1.0 + sim + 0.5 * sim * sim, jnp.float32(0.0))
    denom_parts = jnp.sum(weights, axis=-1)
    numer_parts = jnp.einsum(
        "hts,shv->htv", weights.astype(jnp.bfloat16), values, preferred_element_type=jnp.float32
    )
    return (numer_parts, denom_parts)


def head_sum(part, axis):
    size = lax.axis_size(axis)
    total = part
    step = 1
    while step < size:
        pairs = [(i, i ^ step) for i in range(size)]
        total = total + lax.ppermute(total, axis, pairs)
        step *= 2
    return total


def body(lin_query, lin_key, lin_values, win_query, win_key, win_value, conv_weight, head_gain):
    count = lin_query.shape[0]
    heads = lin_query.shape[1] // FDIM
    queries = lin_query.reshape(count, heads, FDIM)
    keys = lin_key.reshape(count, heads, FDIM)
    values = lin_values.reshape(count, heads, VDIM)
    phi_q = compact_features(queries, True)
    phi_k = compact_features(keys, False)
    feat = phi_k.shape[1]
    local_state = split_dot(phi_k, values)
    local_norm = jnp.sum(phi_k, axis=-1)
    size = lax.axis_size("cc") * lax.axis_size("cx") * lax.axis_size("cz")
    packed = jnp.concatenate([local_state.reshape(-1), local_norm.reshape(-1)])
    used = packed.shape[0]
    quantum = size * 128
    padded = -(-used // quantum) * quantum
    packed = jnp.pad(packed, (0, padded - used))
    prior = exclusive_prefix(packed)
    split = heads * feat * VDIM
    prior_state = prior[:split].reshape(heads, feat, VDIM)
    prior_norm = prior[split:used].reshape(heads, feat)
    start = lax.axis_index(CTX) * count
    rims = passed_along((win_key[count - WIN :], win_value[count - WIN :]), CTX, 1)
    key_ext = jnp.concatenate([rims[0], win_key], axis=0)
    value_ext = jnp.concatenate([rims[1], win_value], axis=0)
    window_out = window_slab(win_query, key_ext, value_ext, start)
    taps = conv_weight.astype(jnp.float32)
    value_f32 = value_ext.astype(jnp.float32)
    conv_out = jnp.zeros((count, value_ext.shape[1]), jnp.float32)
    for tap in range(TAPS):
        conv_out = conv_out + taps[tap][None, :] * value_f32[WIN - tap : WIN - tap + count]
    inner_num, inner_den = inner_causal(queries, keys, values)
    numer = inner_num + jnp.einsum("hft,hfv->htv", phi_q, prior_state, precision=THREE)
    denom = inner_den + jnp.einsum("hft,hf->ht", phi_q, prior_norm, precision=THREE)
    lin_out = jnp.transpose(numer / denom[..., None], (1, 0, 2)).reshape(count, heads * VDIM)
    mixed = head_gain[None, :] * (lin_out + window_out + conv_out)
    squares = jnp.sum(lax.all_gather(jnp.sum(mixed * mixed, axis=-1), "head"), axis=0)
    msq = squares / D
    return (mixed * lax.rsqrt(msq + 1e-06)[:, None]).astype(jnp.bfloat16)


def split_ctx(mesh):
    column = mesh.devices[:, 0]
    xs = len({d.coords[0] for d in column})
    cores = len({d.core_on_chip for d in column})
    zs = column.shape[0] // (xs * cores)
    grid = mesh.devices.reshape(xs, zs, cores, mesh.devices.shape[1])
    return Mesh(grid, ("cx", "cz", "cc", "head"))


def solution(mesh):
    mesh = split_ctx(mesh)
    placed = (
        P(CTX, "head"),
        P(CTX, "head"),
        P(CTX, "head"),
        P(CTX, "head"),
        P(CTX, "head"),
        P(CTX, "head"),
        P(None, "head"),
        P("head"),
    )
    return jax.shard_map(
        body, mesh=mesh, in_specs=placed, out_specs=P(CTX, "head"), check_vma=False
    )
```

```python
import math

import numpy as np
import jax
import jax.numpy as jnp
from jax import lax
from jax.sharding import Mesh, PartitionSpec as P

FDIM = 16
VDIM = 128
WIN = 64
TAPS = 3
D = 2048
HIGH = lax.Precision.HIGHEST
THREE = lax.Precision.HIGH


CTX = ("cx", "cz", "cc")


def passed_along(shard, axis, by):
    length = math.prod(lax.axis_size(a) for a in axis)
    pairs = [(i, i + by) for i in range(length) if 0 <= i + by < length]
    return lax.ppermute(shard, axis, pairs)


def features_outer(x_tok):
    xt = jnp.transpose(x_tok.astype(jnp.float32), (1, 2, 0))
    heads, fdim, count = xt.shape
    ones = jnp.ones((heads, 1, count), jnp.float32)
    outer = (xt[:, :, None, :] * xt[:, None, :, :]).reshape(heads, fdim * fdim, count) * (
        1.0 / math.sqrt(32.0)
    )
    return jnp.concatenate([ones, xt * 0.5, outer], axis=1)


def fold_matrix(fdim, doubled):
    full = 1 + fdim + fdim * fdim
    pairs = [(i, j) for i in range(fdim) for j in range(i, fdim)]
    fold = np.zeros((1 + fdim + len(pairs), full), np.float32)
    for r in range(1 + fdim):
        fold[r, r] = 1.0
    for r, (i, j) in enumerate(pairs):
        fold[1 + fdim + r, 1 + fdim + i * fdim + j] = 1.0
        if doubled and i != j:
            fold[1 + fdim + r, 1 + fdim + j * fdim + i] = 1.0
    return jnp.asarray(fold)


def compact_features(x_tok, doubled):
    full = features_outer(x_tok)
    fold = fold_matrix(x_tok.shape[-1], doubled)
    return jnp.einsum("cf,hft->hct", fold, full, precision=THREE)


def masked_rows(rows, upto):
    keep = jnp.arange(rows.shape[0], dtype=jnp.int32)[:, None] < upto
    return jnp.sum(jnp.where(keep, rows, jnp.float32(0.0)), axis=0)


def exclusive_prefix(flat):
    cores = lax.axis_size("cc")
    core = lax.axis_index("cc")
    chips = lax.axis_size("cx") * lax.axis_size("cz")
    pair = lax.all_gather(flat, "cc")
    below_core = masked_rows(pair, core)
    chip = jnp.sum(pair, axis=0)
    share = lax.dynamic_index_in_dim(chip.reshape(cores, -1), core, 0, False)
    recv = lax.all_to_all(share.reshape(chips, -1), ("cx", "cz"), 0, 0, tiled=True)
    lower = jnp.asarray(np.tril(np.ones((chips, chips), np.float32), -1))
    pref = jnp.dot(lower, recv, precision=HIGH, preferred_element_type=jnp.float32)
    back = lax.all_to_all(pref, ("cx", "cz"), 0, 0, tiled=True)
    shares = lax.all_gather(back.reshape(-1), "cc")
    return shares.reshape(-1) + below_core


def window_slab(query, key_ext, value_ext, start):
    count, width = query.shape
    heads = width // VDIM
    blocks = count // WIN
    qb = query.reshape(blocks, WIN, heads, VDIM)
    keys = jnp.concatenate(
        [
            key_ext[:count].reshape(blocks, WIN, heads, VDIM),
            key_ext[WIN:].reshape(blocks, WIN, heads, VDIM),
        ],
        axis=1,
    )
    vals = jnp.concatenate(
        [
            value_ext[:count].reshape(blocks, WIN, heads, VDIM),
            value_ext[WIN:].reshape(blocks, WIN, heads, VDIM),
        ],
        axis=1,
    )
    scores = jnp.einsum("bihe,bjhe->bhij", qb, keys, preferred_element_type=jnp.float32) * (
        1.0 / math.sqrt(VDIM)
    )
    rows_i = jnp.arange(WIN, dtype=jnp.int32)[:, None]
    cols_j = jnp.arange(2 * WIN, dtype=jnp.int32)[None, :]
    block_ids = jnp.arange(blocks, dtype=jnp.int32)[:, None, None]
    position = start + block_ids * WIN + cols_j[None] - WIN
    allowed = (cols_j > rows_i)[None] & (cols_j <= rows_i + WIN)[None] & (position >= 0)
    allowed = allowed[:, None]
    top = jnp.max(jnp.where(allowed, scores, jnp.float32(-1e30)), axis=-1, keepdims=True)
    prob = jnp.where(allowed, jnp.exp(scores - top), jnp.float32(0.0))
    total = jnp.sum(prob, axis=-1)
    out = jnp.einsum(
        "bhij,bjhe->bihe", prob.astype(jnp.bfloat16), vals, preferred_element_type=jnp.float32
    )
    out = out / jnp.transpose(total, (0, 2, 1))[..., None]
    return out.reshape(count, width)


def inner_causal(queries, keys, values):
    count = queries.shape[0]
    sim = jnp.einsum("thf,shf->hts", queries, keys, preferred_element_type=jnp.float32) * 0.25
    row_pos = jnp.arange(count, dtype=jnp.int32)
    causal = row_pos[:, None] >= row_pos[None, :]
    weights = jnp.where(causal[None], 1.0 + sim + 0.5 * sim * sim, jnp.float32(0.0))
    denom_parts = jnp.sum(weights, axis=-1)
    numer_parts = jnp.einsum(
        "hts,shv->htv", weights.astype(jnp.bfloat16), values, preferred_element_type=jnp.float32
    )
    return (numer_parts, denom_parts)


def head_sum(part, axis):
    size = lax.axis_size(axis)
    total = part
    step = 1
    while step < size:
        pairs = [(i, i ^ step) for i in range(size)]
        total = total + lax.ppermute(total, axis, pairs)
        step *= 2
    return total


def body(lin_query, lin_key, lin_values, win_query, win_key, win_value, conv_weight, head_gain):
    count = lin_query.shape[0]
    heads = lin_query.shape[1] // FDIM
    queries = lin_query.reshape(count, heads, FDIM)
    keys = lin_key.reshape(count, heads, FDIM)
    values = lin_values.reshape(count, heads, VDIM)
    values32 = values.astype(jnp.float32)
    phi_q = compact_features(queries, True)
    phi_k = compact_features(keys, False)
    feat = phi_k.shape[1]
    local_state = jnp.einsum("hft,thv->hfv", phi_k, values32, precision=THREE)
    local_norm = jnp.sum(phi_k, axis=-1)
    size = lax.axis_size("cc") * lax.axis_size("cx") * lax.axis_size("cz")
    packed = jnp.concatenate([local_state.reshape(-1), local_norm.reshape(-1)])
    used = packed.shape[0]
    quantum = size * 128
    padded = -(-used // quantum) * quantum
    packed = jnp.pad(packed, (0, padded - used))
    prior = exclusive_prefix(packed)
    split = heads * feat * VDIM
    prior_state = prior[:split].reshape(heads, feat, VDIM)
    prior_norm = prior[split:used].reshape(heads, feat)
    start = lax.axis_index(CTX) * count
    rims = passed_along(jnp.stack([win_key[count - WIN :], win_value[count - WIN :]]), CTX, 1)
    key_ext = jnp.concatenate([rims[0], win_key], axis=0)
    value_ext = jnp.concatenate([rims[1], win_value], axis=0)
    window_out = window_slab(win_query, key_ext, value_ext, start)
    taps = conv_weight.astype(jnp.float32)
    value_f32 = value_ext.astype(jnp.float32)
    conv_out = jnp.zeros((count, value_ext.shape[1]), jnp.float32)
    for tap in range(TAPS):
        conv_out = conv_out + taps[tap][None, :] * value_f32[WIN - tap : WIN - tap + count]
    inner_num, inner_den = inner_causal(queries, keys, values)
    numer = inner_num + jnp.einsum("hft,hfv->htv", phi_q, prior_state, precision=THREE)
    denom = inner_den + jnp.einsum("hft,hf->ht", phi_q, prior_norm, precision=THREE)
    lin_out = jnp.transpose(numer / denom[..., None], (1, 0, 2)).reshape(count, heads * VDIM)
    mixed = head_gain[None, :] * (lin_out + window_out + conv_out)
    squares = jnp.sum(lax.all_gather(jnp.sum(mixed * mixed, axis=-1), "head"), axis=0)
    msq = squares / D
    return (mixed * lax.rsqrt(msq + 1e-06)[:, None]).astype(jnp.bfloat16)


def split_ctx(mesh):
    column = mesh.devices[:, 0]
    xs = len({d.coords[0] for d in column})
    cores = len({d.core_on_chip for d in column})
    zs = column.shape[0] // (xs * cores)
    grid = mesh.devices.reshape(xs, zs, cores, mesh.devices.shape[1])
    return Mesh(grid, ("cx", "cz", "cc", "head"))


def solution(mesh):
    mesh = split_ctx(mesh)
    placed = (
        P(CTX, "head"),
        P(CTX, "head"),
        P(CTX, "head"),
        P(CTX, "head"),
        P(CTX, "head"),
        P(CTX, "head"),
        P(None, "head"),
        P("head"),
    )
    return jax.shard_map(
        body, mesh=mesh, in_specs=placed, out_specs=P(CTX, "head"), check_vma=False
    )
```

```python
import math

import numpy as np
import jax
import jax.numpy as jnp
from jax import lax
from jax.sharding import Mesh, PartitionSpec as P

FDIM = 16
VDIM = 128
WIN = 64
TAPS = 3
D = 2048
HIGH = lax.Precision.HIGHEST
THREE = lax.Precision.HIGH


CTX = ("cx", "cz", "cc")


def passed_along(shard, axis, by):
    length = math.prod(lax.axis_size(a) for a in axis)
    pairs = [(i, i + by) for i in range(length) if 0 <= i + by < length]
    return lax.ppermute(shard, axis, pairs)


def pair_selectors(fdim, doubled):
    pairs = [(i, j) for i in range(fdim) for j in range(i, fdim)]
    left = np.zeros((len(pairs), fdim), np.float32)
    right = np.zeros((len(pairs), fdim), np.float32)
    for r, (i, j) in enumerate(pairs):
        left[r, i] = 2.0 if (doubled and i != j) else 1.0
        right[r, j] = 1.0
    return jnp.asarray(left, jnp.bfloat16), jnp.asarray(right, jnp.bfloat16)


def compact_features(x_tok, doubled):
    count, heads, fdim = x_tok.shape
    left, right = pair_selectors(fdim, doubled)
    xb = jnp.transpose(x_tok, (1, 2, 0))
    a = jnp.einsum("rf,hft->hrt", left, xb, preferred_element_type=jnp.float32)
    b = jnp.einsum("rf,hft->hrt", right, xb, preferred_element_type=jnp.float32)
    xt = xb.astype(jnp.float32)
    ones = jnp.ones((heads, 1, count), jnp.float32)
    outer = (a * b) * (1.0 / math.sqrt(32.0))
    return jnp.concatenate([ones, xt * 0.5, outer], axis=1)


def split_dot(feats, values):
    hi = feats.astype(jnp.bfloat16)
    lo = (feats - hi.astype(jnp.float32)).astype(jnp.bfloat16)
    first = jnp.einsum("hft,thv->hfv", hi, values, preferred_element_type=jnp.float32)
    second = jnp.einsum("hft,thv->hfv", lo, values, preferred_element_type=jnp.float32)
    return first + second


def masked_rows(rows, upto):
    keep = jnp.arange(rows.shape[0], dtype=jnp.int32)[:, None] < upto
    return jnp.sum(jnp.where(keep, rows, jnp.float32(0.0)), axis=0)


def exclusive_prefix(flat, later):
    cores = lax.axis_size("cc")
    core = lax.axis_index("cc")
    chips = lax.axis_size("cx") * lax.axis_size("cz")
    pair = lax.all_gather(flat, "cc")
    below_core = masked_rows(pair, core)
    halves = pair.reshape(cores, cores, -1)
    share = jnp.sum(lax.dynamic_index_in_dim(halves, core, 1, False), axis=0)
    recv = lax.all_to_all(share.reshape(chips, -1), ("cx", "cz"), 0, 0, tiled=True)
    recv, later = lax.optimization_barrier((recv, later))
    lower = jnp.asarray(np.tril(np.ones((chips, chips), np.float32), -1))
    pref = jnp.dot(lower, recv, precision=HIGH, preferred_element_type=jnp.float32)
    back = lax.all_to_all(pref, ("cx", "cz"), 0, 0, tiled=True)
    shares = lax.all_gather(back.reshape(-1), "cc")
    return shares.reshape(-1) + below_core, later


def window_slab(query, key_ext, value_ext, start):
    count, width = query.shape
    heads = width // VDIM
    blocks = count // WIN
    qb = query.reshape(blocks, WIN, heads, VDIM)
    keys = jnp.concatenate(
        [
            key_ext[:count].reshape(blocks, WIN, heads, VDIM),
            key_ext[WIN:].reshape(blocks, WIN, heads, VDIM),
        ],
        axis=1,
    )
    vals = jnp.concatenate(
        [
            value_ext[:count].reshape(blocks, WIN, heads, VDIM),
            value_ext[WIN:].reshape(blocks, WIN, heads, VDIM),
        ],
        axis=1,
    )
    scores = jnp.einsum("bihe,bjhe->bhij", qb, keys, preferred_element_type=jnp.float32) * (
        1.0 / math.sqrt(VDIM)
    )
    rows_i = jnp.arange(WIN, dtype=jnp.int32)[:, None]
    cols_j = jnp.arange(2 * WIN, dtype=jnp.int32)[None, :]
    block_ids = jnp.arange(blocks, dtype=jnp.int32)[:, None, None]
    position = start + block_ids * WIN + cols_j[None] - WIN
    allowed = (cols_j > rows_i)[None] & (cols_j <= rows_i + WIN)[None] & (position >= 0)
    allowed = allowed[:, None]
    top = jnp.max(jnp.where(allowed, scores, jnp.float32(-1e30)), axis=-1, keepdims=True)
    prob = jnp.where(allowed, jnp.exp(scores - top), jnp.float32(0.0))
    total = jnp.sum(prob, axis=-1)
    out = jnp.einsum(
        "bhij,bjhe->bihe", prob.astype(jnp.bfloat16), vals, preferred_element_type=jnp.float32
    )
    out = out / jnp.transpose(total, (0, 2, 1))[..., None]
    return out.reshape(count, width)


def inner_causal(queries, keys, values):
    count = queries.shape[0]
    sim = jnp.einsum("thf,shf->hts", queries, keys, preferred_element_type=jnp.float32) * 0.25
    row_pos = jnp.arange(count, dtype=jnp.int32)
    causal = row_pos[:, None] >= row_pos[None, :]
    weights = jnp.where(causal[None], 1.0 + sim + 0.5 * sim * sim, jnp.float32(0.0))
    denom_parts = jnp.sum(weights, axis=-1)
    numer_parts = jnp.einsum(
        "hts,shv->htv", weights.astype(jnp.bfloat16), values, preferred_element_type=jnp.float32
    )
    return (numer_parts, denom_parts)


def head_sum(part, axis):
    size = lax.axis_size(axis)
    total = part
    step = 1
    while step < size:
        pairs = [(i, i ^ step) for i in range(size)]
        total = total + lax.ppermute(total, axis, pairs)
        step *= 2
    return total


def body(lin_query, lin_key, lin_values, win_query, win_key, win_value, conv_weight, head_gain):
    count = lin_query.shape[0]
    heads = lin_query.shape[1] // FDIM
    queries = lin_query.reshape(count, heads, FDIM)
    keys = lin_key.reshape(count, heads, FDIM)
    values = lin_values.reshape(count, heads, VDIM)
    phi_q = compact_features(queries, True)
    phi_k = compact_features(keys, False)
    feat = phi_k.shape[1]
    local_state = split_dot(phi_k, values)
    local_norm = jnp.sum(phi_k, axis=-1)
    size = lax.axis_size("cc") * lax.axis_size("cx") * lax.axis_size("cz")
    packed = jnp.concatenate([local_state.reshape(-1), local_norm.reshape(-1)])
    used = packed.shape[0]
    quantum = size * 128
    padded = -(-used // quantum) * quantum
    packed = jnp.pad(packed, (0, padded - used))
    prior, win_query = exclusive_prefix(packed, win_query)
    split = heads * feat * VDIM
    prior_state = prior[:split].reshape(heads, feat, VDIM)
    prior_norm = prior[split:used].reshape(heads, feat)
    start = lax.axis_index(CTX) * count
    rims = passed_along((win_key[count - WIN :], win_value[count - WIN :]), CTX, 1)
    key_ext = jnp.concatenate([rims[0], win_key], axis=0)
    value_ext = jnp.concatenate([rims[1], win_value], axis=0)
    window_out = window_slab(win_query, key_ext, value_ext, start)
    taps = conv_weight.astype(jnp.float32)
    value_f32 = value_ext.astype(jnp.float32)
    conv_out = jnp.zeros((count, value_ext.shape[1]), jnp.float32)
    for tap in range(TAPS):
        conv_out = conv_out + taps[tap][None, :] * value_f32[WIN - tap : WIN - tap + count]
    inner_num, inner_den = inner_causal(queries, keys, values)
    numer = inner_num + jnp.einsum("hft,hfv->htv", phi_q, prior_state, precision=THREE)
    denom = inner_den + jnp.einsum("hft,hf->ht", phi_q, prior_norm, precision=THREE)
    lin_out = jnp.transpose(numer / denom[..., None], (1, 0, 2)).reshape(count, heads * VDIM)
    mixed = head_gain[None, :] * (lin_out + window_out + conv_out)
    squares = jnp.sum(lax.all_gather(jnp.sum(mixed * mixed, axis=-1), "head"), axis=0)
    msq = squares / D
    return (mixed * lax.rsqrt(msq + 1e-06)[:, None]).astype(jnp.bfloat16)


def split_ctx(mesh):
    column = mesh.devices[:, 0]
    xs = len({d.coords[0] for d in column})
    cores = len({d.core_on_chip for d in column})
    zs = column.shape[0] // (xs * cores)
    grid = mesh.devices.reshape(xs, zs, cores, mesh.devices.shape[1])
    return Mesh(grid, ("cx", "cz", "cc", "head"))


def solution(mesh):
    mesh = split_ctx(mesh)
    placed = (
        P(CTX, "head"),
        P(CTX, "head"),
        P(CTX, "head"),
        P(CTX, "head"),
        P(CTX, "head"),
        P(CTX, "head"),
        P(None, "head"),
        P("head"),
    )
    return jax.shard_map(
        body, mesh=mesh, in_specs=placed, out_specs=P(CTX, "head"), check_vma=False
    )
```

```python
import math

import numpy as np
import jax
import jax.numpy as jnp
from jax import lax
from jax.sharding import Mesh, PartitionSpec as P

FDIM = 16
VDIM = 128
WIN = 64
TAPS = 3
D = 2048
HIGH = lax.Precision.HIGHEST
THREE = lax.Precision.HIGH


CTX = ("cx", "cz", "cc")


def passed_along(shard, axis, by):
    length = math.prod(lax.axis_size(a) for a in axis)
    pairs = [(i, i + by) for i in range(length) if 0 <= i + by < length]
    return lax.ppermute(shard, axis, pairs)


def features_outer(x_tok):
    xt = jnp.transpose(x_tok.astype(jnp.float32), (1, 2, 0))
    heads, fdim, count = xt.shape
    ones = jnp.ones((heads, 1, count), jnp.float32)
    outer = (xt[:, :, None, :] * xt[:, None, :, :]).reshape(heads, fdim * fdim, count) * (
        1.0 / math.sqrt(32.0)
    )
    return jnp.concatenate([ones, xt * 0.5, outer], axis=1)


def fold_matrix(fdim, doubled):
    full = 1 + fdim + fdim * fdim
    pairs = [(i, j) for i in range(fdim) for j in range(i, fdim)]
    fold = np.zeros((1 + fdim + len(pairs), full), np.float32)
    for r in range(1 + fdim):
        fold[r, r] = 1.0
    for r, (i, j) in enumerate(pairs):
        fold[1 + fdim + r, 1 + fdim + i * fdim + j] = 1.0
        if doubled and i != j:
            fold[1 + fdim + r, 1 + fdim + j * fdim + i] = 1.0
    return jnp.asarray(fold)


def compact_features(x_tok, doubled):
    full = features_outer(x_tok)
    fold = fold_matrix(x_tok.shape[-1], doubled)
    return jnp.einsum("cf,hft->hct", fold, full, precision=THREE)


def masked_rows(rows, upto):
    keep = jnp.arange(rows.shape[0], dtype=jnp.int32)[:, None] < upto
    return jnp.sum(jnp.where(keep, rows, jnp.float32(0.0)), axis=0)


def exclusive_prefix(flat, later):
    cores = lax.axis_size("cc")
    core = lax.axis_index("cc")
    chips = lax.axis_size("cx") * lax.axis_size("cz")
    pair = lax.all_gather(flat, "cc")
    below_core = masked_rows(pair, core)
    chip = jnp.sum(pair, axis=0)
    share = lax.dynamic_index_in_dim(chip.reshape(cores, -1), core, 0, False)
    recv = lax.all_to_all(share.reshape(chips, -1), ("cx", "cz"), 0, 0, tiled=True)
    recv, later = lax.optimization_barrier((recv, later))
    lower = jnp.asarray(np.tril(np.ones((chips, chips), np.float32), -1))
    pref = jnp.dot(lower, recv, precision=HIGH, preferred_element_type=jnp.float32)
    back = lax.all_to_all(pref, ("cx", "cz"), 0, 0, tiled=True)
    shares = lax.all_gather(back.reshape(-1), "cc")
    return shares.reshape(-1) + below_core, later


def window_slab(query, key_ext, value_ext, start):
    count, width = query.shape
    heads = width // VDIM
    blocks = count // WIN
    qb = query.reshape(blocks, WIN, heads, VDIM)
    keys = jnp.concatenate(
        [
            key_ext[:count].reshape(blocks, WIN, heads, VDIM),
            key_ext[WIN:].reshape(blocks, WIN, heads, VDIM),
        ],
        axis=1,
    )
    vals = jnp.concatenate(
        [
            value_ext[:count].reshape(blocks, WIN, heads, VDIM),
            value_ext[WIN:].reshape(blocks, WIN, heads, VDIM),
        ],
        axis=1,
    )
    scores = jnp.einsum("bihe,bjhe->bhij", qb, keys, preferred_element_type=jnp.float32) * (
        1.0 / math.sqrt(VDIM)
    )
    rows_i = jnp.arange(WIN, dtype=jnp.int32)[:, None]
    cols_j = jnp.arange(2 * WIN, dtype=jnp.int32)[None, :]
    block_ids = jnp.arange(blocks, dtype=jnp.int32)[:, None, None]
    position = start + block_ids * WIN + cols_j[None] - WIN
    allowed = (cols_j > rows_i)[None] & (cols_j <= rows_i + WIN)[None] & (position >= 0)
    allowed = allowed[:, None]
    top = jnp.max(jnp.where(allowed, scores, jnp.float32(-1e30)), axis=-1, keepdims=True)
    prob = jnp.where(allowed, jnp.exp(scores - top), jnp.float32(0.0))
    total = jnp.sum(prob, axis=-1)
    out = jnp.einsum(
        "bhij,bjhe->bihe", prob.astype(jnp.bfloat16), vals, preferred_element_type=jnp.float32
    )
    out = out / jnp.transpose(total, (0, 2, 1))[..., None]
    return out.reshape(count, width)


def inner_causal(queries, keys, values):
    count = queries.shape[0]
    sim = jnp.einsum("thf,shf->hts", queries, keys, preferred_element_type=jnp.float32) * 0.25
    row_pos = jnp.arange(count, dtype=jnp.int32)
    causal = row_pos[:, None] >= row_pos[None, :]
    weights = jnp.where(causal[None], 1.0 + sim + 0.5 * sim * sim, jnp.float32(0.0))
    denom_parts = jnp.sum(weights, axis=-1)
    numer_parts = jnp.einsum(
        "hts,shv->htv", weights.astype(jnp.bfloat16), values, preferred_element_type=jnp.float32
    )
    return (numer_parts, denom_parts)


def head_sum(part, axis):
    size = lax.axis_size(axis)
    total = part
    step = 1
    while step < size:
        pairs = [(i, i ^ step) for i in range(size)]
        total = total + lax.ppermute(total, axis, pairs)
        step *= 2
    return total


def body(lin_query, lin_key, lin_values, win_query, win_key, win_value, conv_weight, head_gain):
    count = lin_query.shape[0]
    heads = lin_query.shape[1] // FDIM
    queries = lin_query.reshape(count, heads, FDIM)
    keys = lin_key.reshape(count, heads, FDIM)
    values = lin_values.reshape(count, heads, VDIM)
    values32 = values.astype(jnp.float32)
    phi_q = compact_features(queries, True)
    phi_k = compact_features(keys, False)
    feat = phi_k.shape[1]
    local_state = jnp.einsum("hft,thv->hfv", phi_k, values32, precision=THREE)
    local_norm = jnp.sum(phi_k, axis=-1)
    size = lax.axis_size("cc") * lax.axis_size("cx") * lax.axis_size("cz")
    packed = jnp.concatenate([local_state.reshape(-1), local_norm.reshape(-1)])
    used = packed.shape[0]
    quantum = size * 128
    padded = -(-used // quantum) * quantum
    packed = jnp.pad(packed, (0, padded - used))
    prior, win_query = exclusive_prefix(packed, win_query)
    split = heads * feat * VDIM
    prior_state = prior[:split].reshape(heads, feat, VDIM)
    prior_norm = prior[split:used].reshape(heads, feat)
    start = lax.axis_index(CTX) * count
    rims = passed_along((win_key[count - WIN :], win_value[count - WIN :]), CTX, 1)
    key_ext = jnp.concatenate([rims[0], win_key], axis=0)
    value_ext = jnp.concatenate([rims[1], win_value], axis=0)
    window_out = window_slab(win_query, key_ext, value_ext, start)
    taps = conv_weight.astype(jnp.float32)
    value_f32 = value_ext.astype(jnp.float32)
    conv_out = jnp.zeros((count, value_ext.shape[1]), jnp.float32)
    for tap in range(TAPS):
        conv_out = conv_out + taps[tap][None, :] * value_f32[WIN - tap : WIN - tap + count]
    inner_num, inner_den = inner_causal(queries, keys, values)
    numer = inner_num + jnp.einsum("hft,hfv->htv", phi_q, prior_state, precision=THREE)
    denom = inner_den + jnp.einsum("hft,hf->ht", phi_q, prior_norm, precision=THREE)
    lin_out = jnp.transpose(numer / denom[..., None], (1, 0, 2)).reshape(count, heads * VDIM)
    mixed = head_gain[None, :] * (lin_out + window_out + conv_out)
    squares = jnp.sum(lax.all_gather(jnp.sum(mixed * mixed, axis=-1), "head"), axis=0)
    msq = squares / D
    return (mixed * lax.rsqrt(msq + 1e-06)[:, None]).astype(jnp.bfloat16)


def split_ctx(mesh):
    column = mesh.devices[:, 0]
    xs = len({d.coords[0] for d in column})
    cores = len({d.core_on_chip for d in column})
    zs = column.shape[0] // (xs * cores)
    grid = mesh.devices.reshape(xs, zs, cores, mesh.devices.shape[1])
    return Mesh(grid, ("cx", "cz", "cc", "head"))


def solution(mesh):
    mesh = split_ctx(mesh)
    placed = (
        P(CTX, "head"),
        P(CTX, "head"),
        P(CTX, "head"),
        P(CTX, "head"),
        P(CTX, "head"),
        P(CTX, "head"),
        P(None, "head"),
        P("head"),
    )
    return jax.shard_map(
        body, mesh=mesh, in_specs=placed, out_specs=P(CTX, "head"), check_vma=False
    )
```

```python
import math

import numpy as np
import jax
import jax.numpy as jnp
from jax import lax
from jax.sharding import Mesh, PartitionSpec as P

FDIM = 16
VDIM = 128
WIN = 64
TAPS = 3
D = 2048
HIGH = lax.Precision.HIGHEST
THREE = lax.Precision.HIGH


CTX = ("cx", "cz", "cc")


def passed_along(shard, axis, by):
    length = math.prod(lax.axis_size(a) for a in axis)
    pairs = [(i, i + by) for i in range(length) if 0 <= i + by < length]
    return lax.ppermute(shard, axis, pairs)


def features_outer(x_tok):
    xt = jnp.transpose(x_tok.astype(jnp.float32), (1, 2, 0))
    heads, fdim, count = xt.shape
    ones = jnp.ones((heads, 1, count), jnp.float32)
    outer = (xt[:, :, None, :] * xt[:, None, :, :]).reshape(heads, fdim * fdim, count) * (
        1.0 / math.sqrt(32.0)
    )
    return jnp.concatenate([ones, xt * 0.5, outer], axis=1)


def fold_matrix(fdim, doubled):
    full = 1 + fdim + fdim * fdim
    pairs = [(i, j) for i in range(fdim) for j in range(i, fdim)]
    fold = np.zeros((1 + fdim + len(pairs), full), np.float32)
    for r in range(1 + fdim):
        fold[r, r] = 1.0
    for r, (i, j) in enumerate(pairs):
        fold[1 + fdim + r, 1 + fdim + i * fdim + j] = 1.0
        if doubled and i != j:
            fold[1 + fdim + r, 1 + fdim + j * fdim + i] = 1.0
    return jnp.asarray(fold)


def compact_features(x_tok, doubled):
    full = features_outer(x_tok)
    fold = fold_matrix(x_tok.shape[-1], doubled)
    return jnp.einsum("cf,hft->hct", fold, full, precision=THREE)


def masked_rows(rows, upto):
    keep = jnp.arange(rows.shape[0], dtype=jnp.int32)[:, None] < upto
    return jnp.sum(jnp.where(keep, rows, jnp.float32(0.0)), axis=0)


def exclusive_prefix(flat, later):
    cores = lax.axis_size("cc")
    core = lax.axis_index("cc")
    chips = lax.axis_size("cx") * lax.axis_size("cz")
    pair = lax.all_gather(flat, "cc")
    below_core = masked_rows(pair, core)
    chip = jnp.sum(pair, axis=0)
    share = lax.dynamic_index_in_dim(chip.reshape(cores, -1), core, 0, False)
    recv = lax.all_to_all(share.reshape(chips, -1), ("cx", "cz"), 0, 0, tiled=True)
    recv, later = lax.optimization_barrier((recv, later))
    lower = jnp.asarray(np.tril(np.ones((chips, chips), np.float32), -1))
    pref = jnp.dot(lower, recv, precision=HIGH, preferred_element_type=jnp.float32)
    back = lax.all_to_all(pref, ("cx", "cz"), 0, 0, tiled=True)
    shares = lax.all_gather(back.reshape(-1), "cc")
    return shares.reshape(-1) + below_core, later


def window_slab(query, key_ext, value_ext, start):
    count, width = query.shape
    heads = width // VDIM
    blocks = count // WIN
    qb = query.reshape(blocks, WIN, heads, VDIM)
    keys = jnp.concatenate(
        [
            key_ext[:count].reshape(blocks, WIN, heads, VDIM),
            key_ext[WIN:].reshape(blocks, WIN, heads, VDIM),
        ],
        axis=1,
    )
    vals = jnp.concatenate(
        [
            value_ext[:count].reshape(blocks, WIN, heads, VDIM),
            value_ext[WIN:].reshape(blocks, WIN, heads, VDIM),
        ],
        axis=1,
    )
    scores = jnp.einsum("bihe,bjhe->bhij", qb, keys, preferred_element_type=jnp.float32) * (
        1.0 / math.sqrt(VDIM)
    )
    rows_i = jnp.arange(WIN, dtype=jnp.int32)[:, None]
    cols_j = jnp.arange(2 * WIN, dtype=jnp.int32)[None, :]
    block_ids = jnp.arange(blocks, dtype=jnp.int32)[:, None, None]
    position = start + block_ids * WIN + cols_j[None] - WIN
    allowed = (cols_j > rows_i)[None] & (cols_j <= rows_i + WIN)[None] & (position >= 0)
    allowed = allowed[:, None]
    top = jnp.max(jnp.where(allowed, scores, jnp.float32(-1e30)), axis=-1, keepdims=True)
    prob = jnp.where(allowed, jnp.exp(scores - top), jnp.float32(0.0))
    total = jnp.sum(prob, axis=-1)
    out = jnp.einsum(
        "bhij,bjhe->bihe", prob.astype(jnp.bfloat16), vals, preferred_element_type=jnp.float32
    )
    out = out / jnp.transpose(total, (0, 2, 1))[..., None]
    return out.reshape(count, width)


def inner_causal(queries, keys, values):
    count = queries.shape[0]
    sim = jnp.einsum("thf,shf->hts", queries, keys, preferred_element_type=jnp.float32) * 0.25
    row_pos = jnp.arange(count, dtype=jnp.int32)
    causal = row_pos[:, None] >= row_pos[None, :]
    weights = jnp.where(causal[None], 1.0 + sim + 0.5 * sim * sim, jnp.float32(0.0))
    denom_parts = jnp.sum(weights, axis=-1)
    numer_parts = jnp.einsum(
        "hts,shv->htv", weights.astype(jnp.bfloat16), values, preferred_element_type=jnp.float32
    )
    return (numer_parts, denom_parts)


def head_sum(part, axis):
    size = lax.axis_size(axis)
    total = part
    step = 1
    while step < size:
        pairs = [(i, i ^ step) for i in range(size)]
        total = total + lax.ppermute(total, axis, pairs)
        step *= 2
    return total


def body(lin_query, lin_key, lin_values, win_query, win_key, win_value, conv_weight, head_gain):
    count = lin_query.shape[0]
    heads = lin_query.shape[1] // FDIM
    queries = lin_query.reshape(count, heads, FDIM)
    keys = lin_key.reshape(count, heads, FDIM)
    values = lin_values.reshape(count, heads, VDIM)
    values32 = values.astype(jnp.float32)
    phi_q = compact_features(queries, True)
    phi_k = compact_features(keys, False)
    feat = phi_k.shape[1]
    local_state = jnp.einsum("hft,thv->hfv", phi_k, values32, precision=THREE)
    local_norm = jnp.sum(phi_k, axis=-1)
    norm_rows = -(-feat // VDIM)
    rows = -(-(feat + norm_rows) // 8) * 8
    norm_block = jnp.pad(local_norm, ((0, 0), (0, norm_rows * VDIM - feat)))
    packed = jnp.concatenate(
        [
            local_state,
            norm_block.reshape(heads, norm_rows, VDIM),
            jnp.zeros((heads, rows - feat - norm_rows, VDIM), jnp.float32),
        ],
        axis=1,
    ).reshape(-1)
    prior, win_query = exclusive_prefix(packed, win_query)
    blocks = prior.reshape(heads, rows, VDIM)
    prior_state = blocks[:, :feat, :]
    prior_norm = blocks[:, feat : feat + norm_rows, :].reshape(heads, -1)[:, :feat]
    start = lax.axis_index(CTX) * count
    rims = passed_along((win_key[count - WIN :], win_value[count - WIN :]), CTX, 1)
    key_ext = jnp.concatenate([rims[0], win_key], axis=0)
    value_ext = jnp.concatenate([rims[1], win_value], axis=0)
    window_out = window_slab(win_query, key_ext, value_ext, start)
    taps = conv_weight.astype(jnp.float32)
    value_f32 = value_ext.astype(jnp.float32)
    conv_out = jnp.zeros((count, value_ext.shape[1]), jnp.float32)
    for tap in range(TAPS):
        conv_out = conv_out + taps[tap][None, :] * value_f32[WIN - tap : WIN - tap + count]
    inner_num, inner_den = inner_causal(queries, keys, values)
    numer = inner_num + jnp.einsum("hft,hfv->htv", phi_q, prior_state, precision=THREE)
    denom = inner_den + jnp.einsum("hft,hf->ht", phi_q, prior_norm, precision=THREE)
    lin_out = jnp.transpose(numer / denom[..., None], (1, 0, 2)).reshape(count, heads * VDIM)
    mixed = head_gain[None, :] * (lin_out + window_out + conv_out)
    squares = jnp.sum(lax.all_gather(jnp.sum(mixed * mixed, axis=-1), "head"), axis=0)
    msq = squares / D
    return (mixed * lax.rsqrt(msq + 1e-06)[:, None]).astype(jnp.bfloat16)


def split_ctx(mesh):
    column = mesh.devices[:, 0]
    xs = len({d.coords[0] for d in column})
    cores = len({d.core_on_chip for d in column})
    zs = column.shape[0] // (xs * cores)
    grid = mesh.devices.reshape(xs, zs, cores, mesh.devices.shape[1])
    return Mesh(grid, ("cx", "cz", "cc", "head"))


def solution(mesh):
    mesh = split_ctx(mesh)
    placed = (
        P(CTX, "head"),
        P(CTX, "head"),
        P(CTX, "head"),
        P(CTX, "head"),
        P(CTX, "head"),
        P(CTX, "head"),
        P(None, "head"),
        P("head"),
    )
    return jax.shard_map(
        body, mesh=mesh, in_specs=placed, out_specs=P(CTX, "head"), check_vma=False
    )
```

```python
import math

import numpy as np
import jax
import jax.numpy as jnp
from jax import lax
from jax.sharding import Mesh, PartitionSpec as P

FDIM = 16
VDIM = 128
WIN = 64
TAPS = 3
D = 2048
HIGH = lax.Precision.HIGHEST
THREE = lax.Precision.HIGH


CTX = ("cx", "cz", "cc")


def passed_along(shard, axis, by):
    length = math.prod(lax.axis_size(a) for a in axis)
    pairs = [(i, i + by) for i in range(length) if 0 <= i + by < length]
    return lax.ppermute(shard, axis, pairs)


def features_outer(x_tok):
    xt = jnp.transpose(x_tok.astype(jnp.float32), (1, 2, 0))
    heads, fdim, count = xt.shape
    ones = jnp.ones((heads, 1, count), jnp.float32)
    outer = (xt[:, :, None, :] * xt[:, None, :, :]).reshape(heads, fdim * fdim, count) * (
        1.0 / math.sqrt(32.0)
    )
    return jnp.concatenate([ones, xt * 0.5, outer], axis=1)


def fold_matrix(fdim, doubled):
    full = 1 + fdim + fdim * fdim
    pairs = [(i, j) for i in range(fdim) for j in range(i, fdim)]
    fold = np.zeros((1 + fdim + len(pairs), full), np.float32)
    for r in range(1 + fdim):
        fold[r, r] = 1.0
    for r, (i, j) in enumerate(pairs):
        fold[1 + fdim + r, 1 + fdim + i * fdim + j] = 1.0
        if doubled and i != j:
            fold[1 + fdim + r, 1 + fdim + j * fdim + i] = 1.0
    return jnp.asarray(fold)


def compact_features(x_tok, doubled):
    full = features_outer(x_tok)
    fold = fold_matrix(x_tok.shape[-1], doubled)
    return jnp.einsum("cf,hft->hct", fold, full, precision=THREE)


def masked_rows(rows, upto):
    keep = jnp.arange(rows.shape[0], dtype=jnp.int32)[:, None] < upto
    return jnp.sum(jnp.where(keep, rows, jnp.float32(0.0)), axis=0)


def exclusive_prefix(flat, later):
    cores = lax.axis_size("cc")
    core = lax.axis_index("cc")
    chips = lax.axis_size("cx") * lax.axis_size("cz")
    pair = lax.all_gather(flat, "cc")
    chip = jnp.sum(pair, axis=0)
    share = lax.dynamic_index_in_dim(chip.reshape(cores, -1), core, 0, False)
    recv = lax.all_to_all(share.reshape(chips, -1), ("cx", "cz"), 0, 0, tiled=True)
    recv, later, pair = lax.optimization_barrier((recv, later, pair))
    below_core = masked_rows(pair, core)
    lower = jnp.asarray(np.tril(np.ones((chips, chips), np.float32), -1))
    pref = jnp.dot(lower, recv, precision=HIGH, preferred_element_type=jnp.float32)
    back = lax.all_to_all(pref, ("cx", "cz"), 0, 0, tiled=True)
    shares = lax.all_gather(back.reshape(-1), "cc")
    return shares.reshape(-1) + below_core, later


def window_slab(query, key_ext, value_ext, start):
    count, width = query.shape
    heads = width // VDIM
    blocks = count // WIN
    qb = query.reshape(blocks, WIN, heads, VDIM)
    keys = jnp.concatenate(
        [
            key_ext[:count].reshape(blocks, WIN, heads, VDIM),
            key_ext[WIN:].reshape(blocks, WIN, heads, VDIM),
        ],
        axis=1,
    )
    vals = jnp.concatenate(
        [
            value_ext[:count].reshape(blocks, WIN, heads, VDIM),
            value_ext[WIN:].reshape(blocks, WIN, heads, VDIM),
        ],
        axis=1,
    )
    scores = jnp.einsum("bihe,bjhe->bhij", qb, keys, preferred_element_type=jnp.float32) * (
        1.0 / math.sqrt(VDIM)
    )
    rows_i = jnp.arange(WIN, dtype=jnp.int32)[:, None]
    cols_j = jnp.arange(2 * WIN, dtype=jnp.int32)[None, :]
    block_ids = jnp.arange(blocks, dtype=jnp.int32)[:, None, None]
    position = start + block_ids * WIN + cols_j[None] - WIN
    allowed = (cols_j > rows_i)[None] & (cols_j <= rows_i + WIN)[None] & (position >= 0)
    allowed = allowed[:, None]
    top = jnp.max(jnp.where(allowed, scores, jnp.float32(-1e30)), axis=-1, keepdims=True)
    prob = jnp.where(allowed, jnp.exp(scores - top), jnp.float32(0.0))
    total = jnp.sum(prob, axis=-1)
    out = jnp.einsum(
        "bhij,bjhe->bihe", prob.astype(jnp.bfloat16), vals, preferred_element_type=jnp.float32
    )
    out = out / jnp.transpose(total, (0, 2, 1))[..., None]
    return out.reshape(count, width)


def inner_causal(queries, keys, values):
    count = queries.shape[0]
    sim = jnp.einsum("thf,shf->hts", queries, keys, preferred_element_type=jnp.float32) * 0.25
    row_pos = jnp.arange(count, dtype=jnp.int32)
    causal = row_pos[:, None] >= row_pos[None, :]
    weights = jnp.where(causal[None], 1.0 + sim + 0.5 * sim * sim, jnp.float32(0.0))
    denom_parts = jnp.sum(weights, axis=-1)
    numer_parts = jnp.einsum(
        "hts,shv->htv", weights.astype(jnp.bfloat16), values, preferred_element_type=jnp.float32
    )
    return (numer_parts, denom_parts)


def head_sum(part, axis):
    size = lax.axis_size(axis)
    total = part
    step = 1
    while step < size:
        pairs = [(i, i ^ step) for i in range(size)]
        total = total + lax.ppermute(total, axis, pairs)
        step *= 2
    return total


def body(lin_query, lin_key, lin_values, win_query, win_key, win_value, conv_weight, head_gain):
    count = lin_query.shape[0]
    heads = lin_query.shape[1] // FDIM
    queries = lin_query.reshape(count, heads, FDIM)
    keys = lin_key.reshape(count, heads, FDIM)
    values = lin_values.reshape(count, heads, VDIM)
    values32 = values.astype(jnp.float32)
    phi_q = compact_features(queries, True)
    phi_k = compact_features(keys, False)
    feat = phi_k.shape[1]
    local_state = jnp.einsum("hft,thv->hfv", phi_k, values32, precision=THREE)
    local_norm = jnp.sum(phi_k, axis=-1)
    size = lax.axis_size("cc") * lax.axis_size("cx") * lax.axis_size("cz")
    packed = jnp.concatenate([local_state.reshape(-1), local_norm.reshape(-1)])
    used = packed.shape[0]
    quantum = size * 128
    padded = -(-used // quantum) * quantum
    packed = jnp.pad(packed, (0, padded - used))
    prior, win_query = exclusive_prefix(packed, win_query)
    split = heads * feat * VDIM
    prior_state = prior[:split].reshape(heads, feat, VDIM)
    prior_norm = prior[split:used].reshape(heads, feat)
    start = lax.axis_index(CTX) * count
    rims = passed_along((win_key[count - WIN :], win_value[count - WIN :]), CTX, 1)
    key_ext = jnp.concatenate([rims[0], win_key], axis=0)
    value_ext = jnp.concatenate([rims[1], win_value], axis=0)
    window_out = window_slab(win_query, key_ext, value_ext, start)
    taps = conv_weight.astype(jnp.float32)
    value_f32 = value_ext.astype(jnp.float32)
    conv_out = jnp.zeros((count, value_ext.shape[1]), jnp.float32)
    for tap in range(TAPS):
        conv_out = conv_out + taps[tap][None, :] * value_f32[WIN - tap : WIN - tap + count]
    inner_num, inner_den = inner_causal(queries, keys, values)
    numer = inner_num + jnp.einsum("hft,hfv->htv", phi_q, prior_state, precision=THREE)
    denom = inner_den + jnp.einsum("hft,hf->ht", phi_q, prior_norm, precision=THREE)
    lin_out = jnp.transpose(numer / denom[..., None], (1, 0, 2)).reshape(count, heads * VDIM)
    mixed = head_gain[None, :] * (lin_out + window_out + conv_out)
    squares = jnp.sum(lax.all_gather(jnp.sum(mixed * mixed, axis=-1), "head"), axis=0)
    msq = squares / D
    return (mixed * lax.rsqrt(msq + 1e-06)[:, None]).astype(jnp.bfloat16)


def split_ctx(mesh):
    column = mesh.devices[:, 0]
    xs = len({d.coords[0] for d in column})
    cores = len({d.core_on_chip for d in column})
    zs = column.shape[0] // (xs * cores)
    grid = mesh.devices.reshape(xs, zs, cores, mesh.devices.shape[1])
    return Mesh(grid, ("cx", "cz", "cc", "head"))


def solution(mesh):
    mesh = split_ctx(mesh)
    placed = (
        P(CTX, "head"),
        P(CTX, "head"),
        P(CTX, "head"),
        P(CTX, "head"),
        P(CTX, "head"),
        P(CTX, "head"),
        P(None, "head"),
        P("head"),
    )
    return jax.shard_map(
        body, mesh=mesh, in_specs=placed, out_specs=P(CTX, "head"), check_vma=False
    )
```

```python
import math

import numpy as np
import jax
import jax.numpy as jnp
from jax import lax
from jax.sharding import Mesh, PartitionSpec as P

FDIM = 16
VDIM = 128
WIN = 64
TAPS = 3
D = 2048
HIGH = lax.Precision.HIGHEST
THREE = lax.Precision.HIGH


CTX = ("cx", "cz", "cc")


def passed_along(shard, axis, by):
    length = math.prod(lax.axis_size(a) for a in axis)
    pairs = [(i, i + by) for i in range(length) if 0 <= i + by < length]
    return lax.ppermute(shard, axis, pairs)


def features_outer(x_tok):
    xt = jnp.transpose(x_tok.astype(jnp.float32), (1, 2, 0))
    heads, fdim, count = xt.shape
    ones = jnp.ones((heads, 1, count), jnp.float32)
    outer = (xt[:, :, None, :] * xt[:, None, :, :]).reshape(heads, fdim * fdim, count) * (
        1.0 / math.sqrt(32.0)
    )
    return jnp.concatenate([ones, xt * 0.5, outer], axis=1)


def fold_matrix(fdim, doubled):
    full = 1 + fdim + fdim * fdim
    pairs = [(i, j) for i in range(fdim) for j in range(i, fdim)]
    fold = np.zeros((1 + fdim + len(pairs), full), np.float32)
    for r in range(1 + fdim):
        fold[r, r] = 1.0
    for r, (i, j) in enumerate(pairs):
        fold[1 + fdim + r, 1 + fdim + i * fdim + j] = 1.0
        if doubled and i != j:
            fold[1 + fdim + r, 1 + fdim + j * fdim + i] = 1.0
    return jnp.asarray(fold)


def compact_features(x_tok, doubled):
    full = features_outer(x_tok)
    fold = fold_matrix(x_tok.shape[-1], doubled)
    return jnp.einsum("cf,hft->hct", fold, full, precision=THREE)


def masked_rows(rows, upto):
    keep = jnp.arange(rows.shape[0], dtype=jnp.int32)[:, None] < upto
    return jnp.sum(jnp.where(keep, rows, jnp.float32(0.0)), axis=0)


def exclusive_prefix(flat, later):
    cores = lax.axis_size("cc")
    core = lax.axis_index("cc")
    chips = lax.axis_size("cx") * lax.axis_size("cz")
    pair = lax.all_gather(flat, "cc")
    below_core = masked_rows(pair, core)
    chip = jnp.sum(pair, axis=0)
    share = lax.dynamic_index_in_dim(chip.reshape(cores, -1), core, 0, False)
    recv = lax.all_to_all(share.reshape(chips, -1), ("cx", "cz"), 0, 0, tiled=True)
    recv, later = lax.optimization_barrier((recv, later))
    lower = jnp.asarray(np.tril(np.ones((chips, chips), np.float32), -1))
    pref = jnp.dot(lower, recv, precision=HIGH, preferred_element_type=jnp.float32)
    back = lax.all_to_all(pref, ("cx", "cz"), 0, 0, tiled=True)
    shares = lax.all_gather(back.reshape(-1), "cc")
    return shares.reshape(-1) + below_core, later


def window_slab(query, key_ext, value_ext, start):
    count, width = query.shape
    heads = width // VDIM
    blocks = count // WIN
    qb = query.reshape(blocks, WIN, heads, VDIM)
    keys = jnp.concatenate(
        [
            key_ext[:count].reshape(blocks, WIN, heads, VDIM),
            key_ext[WIN:].reshape(blocks, WIN, heads, VDIM),
        ],
        axis=1,
    )
    vals = jnp.concatenate(
        [
            value_ext[:count].reshape(blocks, WIN, heads, VDIM),
            value_ext[WIN:].reshape(blocks, WIN, heads, VDIM),
        ],
        axis=1,
    )
    scores = jnp.einsum("bihe,bjhe->bhij", qb, keys, preferred_element_type=jnp.float32) * (
        1.0 / math.sqrt(VDIM)
    )
    rows_i = jnp.arange(WIN, dtype=jnp.int32)[:, None]
    cols_j = jnp.arange(2 * WIN, dtype=jnp.int32)[None, :]
    block_ids = jnp.arange(blocks, dtype=jnp.int32)[:, None, None]
    position = start + block_ids * WIN + cols_j[None] - WIN
    allowed = (cols_j > rows_i)[None] & (cols_j <= rows_i + WIN)[None] & (position >= 0)
    allowed = allowed[:, None]
    top = jnp.max(jnp.where(allowed, scores, jnp.float32(-1e30)), axis=-1, keepdims=True)
    prob = jnp.where(allowed, jnp.exp(scores - top), jnp.float32(0.0))
    total = jnp.sum(prob, axis=-1)
    out = jnp.einsum(
        "bhij,bjhe->bihe", prob.astype(jnp.bfloat16), vals, preferred_element_type=jnp.float32
    )
    out = out / jnp.transpose(total, (0, 2, 1))[..., None]
    return out.reshape(count, width)


def inner_causal(queries, keys, values):
    count = queries.shape[0]
    sim = jnp.einsum("thf,shf->hts", queries, keys, preferred_element_type=jnp.float32) * 0.25
    row_pos = jnp.arange(count, dtype=jnp.int32)
    causal = row_pos[:, None] >= row_pos[None, :]
    weights = jnp.where(causal[None], 1.0 + sim + 0.5 * sim * sim, jnp.float32(0.0))
    denom_parts = jnp.sum(weights, axis=-1)
    numer_parts = jnp.einsum(
        "hts,shv->htv", weights.astype(jnp.bfloat16), values, preferred_element_type=jnp.float32
    )
    return (numer_parts, denom_parts)


def head_sum(part, axis):
    size = lax.axis_size(axis)
    total = part
    step = 1
    while step < size:
        pairs = [(i, i ^ step) for i in range(size)]
        total = total + lax.ppermute(total, axis, pairs)
        step *= 2
    return total


def body(lin_query, lin_key, lin_values, win_query, win_key, win_value, conv_weight, head_gain):
    count = lin_query.shape[0]
    heads = lin_query.shape[1] // FDIM
    queries = lin_query.reshape(count, heads, FDIM)
    keys = lin_key.reshape(count, heads, FDIM)
    values = lin_values.reshape(count, heads, VDIM)
    values32 = values.astype(jnp.float32)
    phi_q = compact_features(queries, True)
    phi_k = compact_features(keys, False)
    feat = phi_k.shape[1]
    local_state = jnp.einsum("hft,thv->hfv", phi_k, values32, precision=THREE)
    local_norm = jnp.sum(phi_k, axis=-1)
    size = lax.axis_size("cc") * lax.axis_size("cx") * lax.axis_size("cz")
    packed = jnp.concatenate([local_state.reshape(-1), local_norm.reshape(-1)])
    used = packed.shape[0]
    quantum = size * 128
    padded = -(-used // quantum) * quantum
    packed = jnp.pad(packed, (0, padded - used))
    prior, (win_query, lin_q_late, lin_k_late) = exclusive_prefix(packed, (win_query, queries, keys))
    split = heads * feat * VDIM
    prior_state = prior[:split].reshape(heads, feat, VDIM)
    prior_norm = prior[split:used].reshape(heads, feat)
    start = lax.axis_index(CTX) * count
    rims = passed_along((win_key[count - WIN :], win_value[count - WIN :]), CTX, 1)
    key_ext = jnp.concatenate([rims[0], win_key], axis=0)
    value_ext = jnp.concatenate([rims[1], win_value], axis=0)
    window_out = window_slab(win_query, key_ext, value_ext, start)
    taps = conv_weight.astype(jnp.float32)
    value_f32 = value_ext.astype(jnp.float32)
    conv_out = jnp.zeros((count, value_ext.shape[1]), jnp.float32)
    for tap in range(TAPS):
        conv_out = conv_out + taps[tap][None, :] * value_f32[WIN - tap : WIN - tap + count]
    inner_num, inner_den = inner_causal(lin_q_late, lin_k_late, values)
    numer = inner_num + jnp.einsum("hft,hfv->htv", phi_q, prior_state, precision=THREE)
    denom = inner_den + jnp.einsum("hft,hf->ht", phi_q, prior_norm, precision=THREE)
    lin_out = jnp.transpose(numer / denom[..., None], (1, 0, 2)).reshape(count, heads * VDIM)
    mixed = head_gain[None, :] * (lin_out + window_out + conv_out)
    squares = jnp.sum(lax.all_gather(jnp.sum(mixed * mixed, axis=-1), "head"), axis=0)
    msq = squares / D
    return (mixed * lax.rsqrt(msq + 1e-06)[:, None]).astype(jnp.bfloat16)


def split_ctx(mesh):
    column = mesh.devices[:, 0]
    xs = len({d.coords[0] for d in column})
    cores = len({d.core_on_chip for d in column})
    zs = column.shape[0] // (xs * cores)
    grid = mesh.devices.reshape(xs, zs, cores, mesh.devices.shape[1])
    return Mesh(grid, ("cx", "cz", "cc", "head"))


def solution(mesh):
    mesh = split_ctx(mesh)
    placed = (
        P(CTX, "head"),
        P(CTX, "head"),
        P(CTX, "head"),
        P(CTX, "head"),
        P(CTX, "head"),
        P(CTX, "head"),
        P(None, "head"),
        P("head"),
    )
    return jax.shard_map(
        body, mesh=mesh, in_specs=placed, out_specs=P(CTX, "head"), check_vma=False
    )
```

```python
import math

import numpy as np
import jax
import jax.numpy as jnp
from jax import lax
from jax.sharding import Mesh, PartitionSpec as P

FDIM = 16
VDIM = 128
WIN = 64
TAPS = 3
D = 2048
HIGH = lax.Precision.HIGHEST
THREE = lax.Precision.HIGH


CTX = ("cx", "cz", "cc")


def passed_along(shard, axis, by):
    length = math.prod(lax.axis_size(a) for a in axis)
    pairs = [(i, i + by) for i in range(length) if 0 <= i + by < length]
    return lax.ppermute(shard, axis, pairs)


def features_outer(x_tok):
    xt = jnp.transpose(x_tok.astype(jnp.float32), (1, 2, 0))
    heads, fdim, count = xt.shape
    ones = jnp.ones((heads, 1, count), jnp.float32)
    outer = (xt[:, :, None, :] * xt[:, None, :, :]).reshape(heads, fdim * fdim, count) * (
        1.0 / math.sqrt(32.0)
    )
    return jnp.concatenate([ones, xt * 0.5, outer], axis=1)


def fold_matrix(fdim, doubled):
    full = 1 + fdim + fdim * fdim
    pairs = [(i, j) for i in range(fdim) for j in range(i, fdim)]
    fold = np.zeros((1 + fdim + len(pairs), full), np.float32)
    for r in range(1 + fdim):
        fold[r, r] = 1.0
    for r, (i, j) in enumerate(pairs):
        fold[1 + fdim + r, 1 + fdim + i * fdim + j] = 1.0
        if doubled and i != j:
            fold[1 + fdim + r, 1 + fdim + j * fdim + i] = 1.0
    return jnp.asarray(fold)


def compact_features(x_tok, doubled):
    full = features_outer(x_tok)
    fold = fold_matrix(x_tok.shape[-1], doubled)
    return jnp.einsum("cf,hft->hct", fold, full, precision=THREE)


def masked_rows(rows, upto):
    keep = jnp.arange(rows.shape[0], dtype=jnp.int32)[:, None] < upto
    return jnp.sum(jnp.where(keep, rows, jnp.float32(0.0)), axis=0)


def exclusive_prefix(flat, later):
    cores = lax.axis_size("cc")
    core = lax.axis_index("cc")
    chips = lax.axis_size("cx") * lax.axis_size("cz")
    pair = lax.all_gather(flat, "cc")
    below_core = masked_rows(pair, core)
    chip = jnp.sum(pair, axis=0)
    share = lax.dynamic_index_in_dim(chip.reshape(cores, -1), core, 0, False)
    recv = lax.all_to_all(share.reshape(chips, -1), ("cx", "cz"), 0, 0, tiled=True)
    recv, later = lax.optimization_barrier((recv, later))
    lower = jnp.asarray(np.tril(np.ones((chips, chips), np.float32), -1))
    pref = jnp.dot(lower, recv, precision=HIGH, preferred_element_type=jnp.float32)
    back = lax.all_to_all(pref, ("cx", "cz"), 0, 0, tiled=True)
    shares = lax.all_gather(back.reshape(-1), "cc")
    return shares.reshape(-1) + below_core, later


def window_slab(query, key_ext, value_ext, start):
    count, width = query.shape
    heads = width // VDIM
    blocks = count // WIN
    qb = query.reshape(blocks, WIN, heads, VDIM)
    keys = jnp.concatenate(
        [
            key_ext[:count].reshape(blocks, WIN, heads, VDIM),
            key_ext[WIN:].reshape(blocks, WIN, heads, VDIM),
        ],
        axis=1,
    )
    vals = jnp.concatenate(
        [
            value_ext[:count].reshape(blocks, WIN, heads, VDIM),
            value_ext[WIN:].reshape(blocks, WIN, heads, VDIM),
        ],
        axis=1,
    )
    scores = jnp.einsum("bihe,bjhe->bhij", qb, keys, preferred_element_type=jnp.float32) * (
        1.0 / math.sqrt(VDIM)
    )
    rows_i = jnp.arange(WIN, dtype=jnp.int32)[:, None]
    cols_j = jnp.arange(2 * WIN, dtype=jnp.int32)[None, :]
    block_ids = jnp.arange(blocks, dtype=jnp.int32)[:, None, None]
    position = start + block_ids * WIN + cols_j[None] - WIN
    allowed = (cols_j > rows_i)[None] & (cols_j <= rows_i + WIN)[None] & (position >= 0)
    allowed = allowed[:, None]
    top = jnp.max(jnp.where(allowed, scores, jnp.float32(-1e30)), axis=-1, keepdims=True)
    prob = jnp.where(allowed, jnp.exp(scores - top), jnp.float32(0.0))
    total = jnp.sum(prob, axis=-1)
    out = jnp.einsum(
        "bhij,bjhe->bihe", prob.astype(jnp.bfloat16), vals, preferred_element_type=jnp.float32
    )
    out = out / jnp.transpose(total, (0, 2, 1))[..., None]
    return out.reshape(count, width)


def inner_causal(queries, keys, values):
    count = queries.shape[0]
    sim = jnp.einsum("thf,shf->hts", queries, keys, preferred_element_type=jnp.float32) * 0.25
    row_pos = jnp.arange(count, dtype=jnp.int32)
    causal = row_pos[:, None] >= row_pos[None, :]
    weights = jnp.where(causal[None], 1.0 + sim + 0.5 * sim * sim, jnp.float32(0.0))
    denom_parts = jnp.sum(weights, axis=-1)
    numer_parts = jnp.einsum(
        "hts,shv->htv", weights.astype(jnp.bfloat16), values, preferred_element_type=jnp.float32
    )
    return (numer_parts, denom_parts)


def head_sum(part, axis):
    size = lax.axis_size(axis)
    total = part
    step = 1
    while step < size:
        pairs = [(i, i ^ step) for i in range(size)]
        total = total + lax.ppermute(total, axis, pairs)
        step *= 2
    return total


def body(lin_query, lin_key, lin_values, win_query, win_key, win_value, conv_weight, head_gain):
    count = lin_query.shape[0]
    heads = lin_query.shape[1] // FDIM
    queries = lin_query.reshape(count, heads, FDIM)
    keys = lin_key.reshape(count, heads, FDIM)
    values = lin_values.reshape(count, heads, VDIM)
    values32 = values.astype(jnp.float32)
    phi_q = compact_features(queries, True)
    phi_k = compact_features(keys, False)
    feat = phi_k.shape[1]
    local_state = jnp.einsum("hft,thv->hfv", phi_k, values32, precision=THREE)
    local_norm = jnp.sum(phi_k, axis=-1)
    size = lax.axis_size("cc") * lax.axis_size("cx") * lax.axis_size("cz")
    packed = jnp.concatenate([local_state.reshape(-1), local_norm.reshape(-1)])
    used = packed.shape[0]
    quantum = size * 128
    padded = -(-used // quantum) * quantum
    packed = jnp.pad(packed, (0, padded - used))
    prior, win_query = exclusive_prefix(packed, win_query)
    split = heads * feat * VDIM
    prior_state = prior[:split].reshape(heads, feat, VDIM)
    prior_norm = prior[split:used].reshape(heads, feat)
    start = lax.axis_index(CTX) * count
    rims = passed_along((win_key[count - WIN :], win_value[count - WIN :]), CTX, 1)
    key_ext = jnp.concatenate([rims[0], win_key], axis=0)
    value_ext = jnp.concatenate([rims[1], win_value], axis=0)
    window_out = window_slab(win_query, key_ext, value_ext, start)
    taps = conv_weight.astype(jnp.float32)
    value_f32 = value_ext.astype(jnp.float32)
    conv_out = jnp.zeros((count, value_ext.shape[1]), jnp.float32)
    for tap in range(TAPS):
        conv_out = conv_out + taps[tap][None, :] * value_f32[WIN - tap : WIN - tap + count]
    inner_num, inner_den = inner_causal(queries, keys, values)
    numer = inner_num + jnp.einsum("hft,hfv->htv", phi_q, prior_state, precision=THREE)
    denom = inner_den + jnp.einsum("hft,hf->ht", phi_q, prior_norm, precision=THREE)
    lin_out = jnp.transpose(numer / denom[..., None], (1, 0, 2)).reshape(count, heads * VDIM)
    mixed = head_gain[None, :] * (lin_out + window_out + conv_out)
    squares = lax.psum(jnp.sum(mixed * mixed, axis=-1), "head")
    msq = squares / D
    return (mixed * lax.rsqrt(msq + 1e-06)[:, None]).astype(jnp.bfloat16)


def split_ctx(mesh):
    column = mesh.devices[:, 0]
    xs = len({d.coords[0] for d in column})
    cores = len({d.core_on_chip for d in column})
    zs = column.shape[0] // (xs * cores)
    grid = mesh.devices.reshape(xs, zs, cores, mesh.devices.shape[1])
    return Mesh(grid, ("cx", "cz", "cc", "head"))


def solution(mesh):
    mesh = split_ctx(mesh)
    placed = (
        P(CTX, "head"),
        P(CTX, "head"),
        P(CTX, "head"),
        P(CTX, "head"),
        P(CTX, "head"),
        P(CTX, "head"),
        P(None, "head"),
        P("head"),
    )
    return jax.shard_map(
        body, mesh=mesh, in_specs=placed, out_specs=P(CTX, "head"), check_vma=False
    )
```
